32 devices in a mesh: grp: 2 (over y), tile: 4 (over z), freq: 4 (over x, core).
Axes of the slice: x: 2, y: 2, z: 4, core: 2. Of those that a mesh axis runs over, the one named last changes fastest.
Arguments:
- sources: bfloat16 [4, 4, 2048, 512], P('freq', 'grp', 'tile'), parts along dimension 1, may hold values from -6 to 6
- v_factors: bfloat16 [4, 4, 2, 4, 112, 512], P('freq', 'tile', None, 'grp'), parts along dimension 3, may hold values from -0.1875 to 0.1875
- u_factors: bfloat16 [4, 4, 4, 112, 1024], P('freq', None, 'grp', None, 'tile'), parts along dimension 2, may hold values from -0.1875 to 0.1875
- tile_ranks: int32 [4, 4, 4], P('freq', 'grp', 'tile'), parts along dimension 1, may hold values from 16 to 112, as said below
- window_bounds: int32 [4, 1024, 512], P('grp', ('tile', 'freq')), parts along dimension 0, may hold values from 0 to 31, as said below
Outputs:
- windowed_traces: float32 [1024, 64, 512], P(('tile', 'freq'), 'grp'), parts along dimension 1
The draws below stay inside these ranges and needn't reach their ends.
There are 2 independent parts, one for each index of `grp`. The reference program is written for one: setup_inputs(seed, part) draws one part's arguments, and reference() takes and returns one part's arrays. A program takes and returns all parts, laid end to end along the dimension named above; each array names one. Nothing has to cross between parts.
Inputs may be any that keep to these rules, and one draw needn't show every extreme that they name: `tile_ranks`: each tile's rank for each frequency; rank slots at or beyond it carry no coefficients. window_bounds[1] - window_bounds[0] lies between 8 and 16 for every receiver and virtual source.
All inputs are finite; a program needn't handle non-finite values.
Results may differ from the reference program's by a relative error of at most 0.0041.
Values may be sent and summed in bfloat16 or wider, within the bound.
No kernel may reach another device: no remote copies, remote signals or barrier semaphores. Data moves between devices by JAX's collectives and lax.ppermute only.
A program may use at most 64 MiB of HBM per device.

```python
import math
import jax
import jax.numpy as jnp
from jax import lax

B = 512
RMAX = 112
RMIN = 16
S = 512
NT = 32
FREQ = 4
TC = 4
TR = 2
SRC = 2048
REC = 1024


def draw_tile_ranks(key, part):
    tile_total = FREQ * TR * TC
    drawn_ranks = jax.random.randint(jax.random.fold_in(key, 11), (tile_total,), RMIN, RMAX + 1)
    positions = jax.random.permutation(jax.random.fold_in(key, 12), tile_total)
    flat_index = jnp.arange(tile_total)
    drawn_ranks = jnp.where(flat_index == positions[0], RMAX, drawn_ranks)
    drawn_ranks = jnp.where(flat_index == positions[1], RMIN, drawn_ranks)
    return drawn_ranks.reshape(FREQ, TR, TC).astype(jnp.int32)


def draw_window_bounds(key, part):
    lower_edge = jax.random.randint(jax.random.fold_in(key, 21), (REC, S), 0, NT // 2)
    spread = jax.random.randint(jax.random.fold_in(key, 22), (REC, S), NT // 4, NT // 2 + 1)
    chosen = jax.random.randint(jax.random.fold_in(key, 23), (), 0, REC * S)
    second_spot = (chosen + 1) % (REC * S)
    flat_index = jnp.arange(REC * S).reshape(REC, S)
    lower_edge = jnp.where(flat_index == chosen, NT // 2 - 1, lower_edge)
    spread = jnp.where(flat_index == chosen, NT // 2, spread)
    lower_edge = jnp.where(flat_index == second_spot, 0, lower_edge)
    upper_edge = lower_edge + spread
    return jnp.stack([lower_edge, upper_edge], axis=0).astype(jnp.int32)


def block_scale(own_key, dims, split, smallest, largest):
    factor_of = 1.0
    for position, blocks in split:
        steps = jax.random.uniform(jax.random.fold_in(jax.random.fold_in(own_key, 6), position), (blocks,), jnp.float32, smallest / len(split), largest / len(split))
        factor_of = factor_of * jnp.repeat(jnp.exp(steps), dims[position] // blocks).reshape((-1,) + (1,) * (len(dims) - 1 - position))
    return factor_of


def normal_values(own_key, shape, deviation, reach, split=(), held_as=jnp.bfloat16):
    loudness = block_scale(own_key, shape, split, -0.22, 0.18) if split else 1.0
    values = jax.random.normal(own_key, shape, jnp.float32) * deviation * loudness
    return jnp.minimum(jnp.maximum(values, -reach), reach).astype(held_as)


def setup_inputs(seed: int = 0, part: int = 0) -> dict:
    keys = jax.random.split(jax.random.key(seed), 6)
    part_splits = jax.random.split(jax.random.fold_in(keys[5], part), 6)
    sources = normal_values(part_splits[0], (FREQ, 2, SRC, S), 1.0, 6.0, ((0, 4), (2, 4)))
    v_factors = normal_values(part_splits[1], (FREQ, TC, TR, 2, RMAX, B), (2 * B) ** -0.5, 0.1875, ((0, 4), (1, 4)))
    u_factors = normal_values(part_splits[2], (FREQ, TC, 2, RMAX, REC), (2 * TC * RMAX) ** -0.5, 0.1875, ((0, 4), (4, 4)))
    tile_ranks = draw_tile_ranks(jax.random.fold_in(jax.random.fold_in(keys[5], part), 71), part)
    window_bounds = draw_window_bounds(jax.random.fold_in(jax.random.fold_in(keys[5], part), 71), part)
    return {"sources": sources, "v_factors": v_factors, "u_factors": u_factors, "tile_ranks": tile_ranks, "window_bounds": window_bounds}


first_bin = 2
highest = lax.Precision.HIGHEST

def inverse_tables(count_freq, count_time):
    freq_index = jnp.arange(count_freq, dtype=jnp.int32)[:, None] + first_bin
    time_index = jnp.arange(count_time, dtype=jnp.int32)[None, :]
    phase_step = freq_index * time_index % count_time
    angles = phase_step.astype(jnp.float32) * (2.0 * math.pi / count_time)
    return (jnp.cos(angles), jnp.sin(angles))

def column_coefficients(packed):
    v_column, x_column, rank_column = packed
    products = jnp.einsum('icrb,dbs->icrds', v_column.astype(jnp.float32), x_column.astype(jnp.float32), precision=highest)
    coef_real = products[:, 0, :, 0] - products[:, 1, :, 1]
    coef_imag = products[:, 0, :, 1] + products[:, 1, :, 0]
    slot_index = jnp.arange(RMAX, dtype=jnp.int32)
    live_slots = (slot_index[None, :] < rank_column[:, None])[:, None, :, None]
    stacked = jnp.stack([coef_real, coef_imag], axis=1)
    return jnp.where(live_slots, stacked, jnp.float32(0.0)).astype(jnp.bfloat16)

def row_spectrum(packed):
    u_row, c_row = packed
    products = jnp.einsum('jcrb,jdrs->cbds', u_row.astype(jnp.float32), c_row.astype(jnp.float32), precision=highest)
    real_part = products[0, :, 0] - products[1, :, 1]
    imag_part = products[0, :, 1] + products[1, :, 0]
    return jnp.stack([real_part, imag_part], axis=0).astype(jnp.bfloat16)

def one_frequency(packed):
    v_freq, u_freq, x_freq, rank_freq = packed
    x_columns = x_freq.reshape(2, TC, B, S).transpose(1, 0, 2, 3)
    coefficients = lax.map(column_coefficients, (v_freq, x_columns, rank_freq.T))
    u_rows = u_freq.reshape(TC, 2, RMAX, TR, B).transpose(3, 0, 1, 2, 4)
    spectra = lax.map(row_spectrum, (u_rows, coefficients.transpose(1, 0, 2, 3, 4)))
    return spectra.transpose(1, 0, 2, 3).reshape(2, TR * B, S)

def reference(sources, v_factors, u_factors, tile_ranks, window_bounds):
    spectra = lax.map(one_frequency, (v_factors, u_factors, sources, tile_ranks))
    cosine_table, sine_table = inverse_tables(FREQ, NT)
    widened = spectra.astype(jnp.float32)
    traces = jnp.einsum('frs,fn->rns', widened[:, 0], cosine_table, precision=highest) - jnp.einsum('frs,fn->rns', widened[:, 1], sine_table, precision=highest)
    traces = traces * (1.0 / math.sqrt(FREQ))
    time_index = jnp.arange(NT, dtype=jnp.int32)[None, :, None]
    inside = (time_index >= window_bounds[0][:, None, :]) & (time_index < window_bounds[1][:, None, :])
    return jnp.where(inside, traces, jnp.float32(0.0)).astype(jnp.float32)
```

```python
import math

import jax
import jax.numpy as jnp
from jax import lax
from jax.sharding import PartitionSpec as P

NT = 32
S_CHUNKS = 1


first_bin = 2


def inverse_tables(count_freq, count_time):
    freq_index = jnp.arange(count_freq, dtype=jnp.int32)[:, None] + first_bin
    time_index = jnp.arange(count_time, dtype=jnp.int32)[None, :]
    phase_step = freq_index * time_index % count_time
    angles = phase_step.astype(jnp.float32) * (2.0 * math.pi / count_time)
    return (jnp.cos(angles), jnp.sin(angles))


def column_products(v_local, x_local, rank_local):
    products = lax.dot_general(
        v_local, x_local, (((3,), (1,)), ((), ())), preferred_element_type=jnp.float32
    )
    coef_real = products[:, 0, :, 0] - products[:, 1, :, 1]
    coef_imag = products[:, 0, :, 1] + products[:, 1, :, 0]
    slot_index = jnp.arange(v_local.shape[2], dtype=jnp.int32)
    live_slots = slot_index[None, :, None] < rank_local[:, None, None]
    coef_real = jnp.where(live_slots, coef_real, jnp.float32(0.0)).astype(jnp.bfloat16)
    coef_imag = jnp.where(live_slots, coef_imag, jnp.float32(0.0)).astype(jnp.bfloat16)
    return jnp.stack([coef_real, coef_imag], axis=1)


def row_spectrum(u_local, blocks):
    products = lax.dot_general(
        u_local, blocks, (((0, 2), (0, 2)), ((), ())), preferred_element_type=jnp.float32
    )
    real_part = products[0, :, 0] - products[1, :, 1]
    imag_part = products[0, :, 1] + products[1, :, 0]
    return jnp.stack([real_part, imag_part], axis=0).astype(jnp.bfloat16)


def relay_exchange(own, u_local):
    t = lax.axis_index("tile")
    up = [(0, 1), (1, 2), (2, 3)]
    down = [(1, 0), (2, 1), (3, 2)]
    up1 = lax.ppermute(own[1], "tile", up)
    down1 = lax.ppermute(own[0], "tile", down)
    up2 = lax.ppermute(jnp.where(t == 0, own[0], up1), "tile", up)
    down2 = lax.ppermute(jnp.where(t == 3, own[1], down1), "tile", down)
    up3 = lax.ppermute(up2, "tile", [(2, 3)])
    down3 = lax.ppermute(down2, "tile", [(1, 0)])
    orders = (
        lambda: (own[0], down1, down2, down3),
        lambda: (up2, own[0], down1, down2),
        lambda: (up2, up1, own[1], down2),
        lambda: (up3, up2, up1, own[1]),
    )
    branches = [
        (lambda order: (lambda: row_spectrum(u_local, jnp.stack(order(), axis=0))))(order)
        for order in orders
    ]
    return lax.switch(t, branches)


def gather_exchange(own, u_local, n_tile):
    repeat = n_tile // own.shape[0]
    sending = jnp.repeat(own, repeat, axis=0)
    received = lax.all_to_all(sending, "tile", split_axis=0, concat_axis=0, tiled=True)
    return row_spectrum(u_local, received)


def make_per_device(n_tile):
    def per_device(sources, v_factors, u_factors, tile_ranks, window_bounds):
        v_local = v_factors[0, 0]
        u_local = u_factors[0]
        x_local = sources[0]
        rank_local = tile_ranks[0, :, 0]
        rows = v_local.shape[0]
        use_relay = n_tile == 4 and rows == 2 and u_local.shape[0] == 4
        count_s = x_local.shape[2]
        chunks = S_CHUNKS if count_s % S_CHUNKS == 0 else 1
        width = count_s // chunks
        received_parts = []
        for c in range(chunks):
            x_part = x_local[:, :, c * width:(c + 1) * width]
            own = column_products(v_local, x_part, rank_local)
            if use_relay:
                spectrum = relay_exchange(own, u_local)
            else:
                spectrum = gather_exchange(own, u_local, n_tile)
            received_parts.append(
                lax.all_to_all(spectrum[None], "freq", split_axis=2, concat_axis=0, tiled=True)
            )
        received = jnp.concatenate(received_parts, axis=3) if chunks > 1 else received_parts[0]
        count_freq = received.shape[0]
        cosine_table, sine_table = inverse_tables(count_freq, NT)
        widened = received.astype(jnp.float32)
        real_sum = 0.0
        imag_sum = 0.0
        for f in range(count_freq):
            real_sum = real_sum + widened[f, 0][:, None, :] * cosine_table[f][None, :, None]
            imag_sum = imag_sum + widened[f, 1][:, None, :] * sine_table[f][None, :, None]
        traces = (real_sum - imag_sum) * (1.0 / math.sqrt(count_freq))
        time_index = jnp.arange(NT, dtype=jnp.int32)[None, :, None]
        inside = (time_index >= window_bounds[0][:, None, :]) & (
            time_index < window_bounds[1][:, None, :]
        )
        return jnp.where(inside, traces, jnp.float32(0.0))

    return per_device


def solution(mesh):
    return jax.shard_map(
        make_per_device(mesh.shape["tile"]),
        mesh=mesh,
        in_specs=(
            P("freq", "grp", "tile", None),
            P("freq", "tile", None, "grp", None, None),
            P("freq", None, "grp", None, "tile"),
            P("freq", "grp", "tile"),
            P("grp", ("tile", "freq"), None),
        ),
        out_specs=P(("tile", "freq"), "grp", None),
        check_vma=False,
    )
```

```python
import math

import jax
import jax.numpy as jnp
from jax import lax
from jax.sharding import PartitionSpec as P

NT = 32
S_CHUNKS = 2


first_bin = 2


def inverse_tables(count_freq, count_time):
    freq_index = jnp.arange(count_freq, dtype=jnp.int32)[:, None] + first_bin
    time_index = jnp.arange(count_time, dtype=jnp.int32)[None, :]
    phase_step = freq_index * time_index % count_time
    angles = phase_step.astype(jnp.float32) * (2.0 * math.pi / count_time)
    return (jnp.cos(angles), jnp.sin(angles))


def column_products(v_local, x_local, rank_local):
    products = lax.dot_general(
        v_local, x_local, (((3,), (1,)), ((), ())), preferred_element_type=jnp.float32
    )
    coef_real = products[:, 0, :, 0] - products[:, 1, :, 1]
    coef_imag = products[:, 0, :, 1] + products[:, 1, :, 0]
    slot_index = jnp.arange(v_local.shape[2], dtype=jnp.int32)
    live_slots = slot_index[None, :, None] < rank_local[:, None, None]
    coef_real = jnp.where(live_slots, coef_real, jnp.float32(0.0)).astype(jnp.bfloat16)
    coef_imag = jnp.where(live_slots, coef_imag, jnp.float32(0.0)).astype(jnp.bfloat16)
    return jnp.stack([coef_real, coef_imag], axis=1)


def row_spectrum(u_local, blocks):
    products = lax.dot_general(
        u_local, blocks, (((0, 2), (0, 2)), ((), ())), preferred_element_type=jnp.float32
    )
    real_part = products[0, :, 0] - products[1, :, 1]
    imag_part = products[0, :, 1] + products[1, :, 0]
    return jnp.stack([real_part, imag_part], axis=0).astype(jnp.bfloat16)


def relay_exchange(own, u_local):
    t = lax.axis_index("tile")
    up = [(0, 1), (1, 2), (2, 3)]
    down = [(1, 0), (2, 1), (3, 2)]
    up1 = lax.ppermute(own[1], "tile", up)
    down1 = lax.ppermute(own[0], "tile", down)
    up2 = lax.ppermute(jnp.where(t == 0, own[0], up1), "tile", up)
    down2 = lax.ppermute(jnp.where(t == 3, own[1], down1), "tile", down)
    up3 = lax.ppermute(up2, "tile", [(2, 3)])
    down3 = lax.ppermute(down2, "tile", [(1, 0)])
    orders = (
        lambda: (own[0], down1, down2, down3),
        lambda: (up2, own[0], down1, down2),
        lambda: (up2, up1, own[1], down2),
        lambda: (up3, up2, up1, own[1]),
    )
    branches = [
        (lambda order: (lambda: row_spectrum(u_local, jnp.stack(order(), axis=0))))(order)
        for order in orders
    ]
    return lax.switch(t, branches)


def gather_exchange(own, u_local, n_tile):
    repeat = n_tile // own.shape[0]
    sending = jnp.repeat(own, repeat, axis=0)
    received = lax.all_to_all(sending, "tile", split_axis=0, concat_axis=0, tiled=True)
    return row_spectrum(u_local, received)


def make_per_device(n_tile):
    def per_device(sources, v_factors, u_factors, tile_ranks, window_bounds):
        v_local = v_factors[0, 0]
        u_local = u_factors[0]
        x_local = sources[0]
        rank_local = tile_ranks[0, :, 0]
        rows = v_local.shape[0]
        use_relay = n_tile == 4 and rows == 2 and u_local.shape[0] == 4
        count_s = x_local.shape[2]
        chunks = S_CHUNKS if count_s % S_CHUNKS == 0 else 1
        width = count_s // chunks
        received_parts = []
        for c in range(chunks):
            x_part = x_local[:, :, c * width:(c + 1) * width]
            own = column_products(v_local, x_part, rank_local)
            if use_relay:
                spectrum = relay_exchange(own, u_local)
            else:
                spectrum = gather_exchange(own, u_local, n_tile)
            received_parts.append(
                lax.all_to_all(spectrum[None], "freq", split_axis=2, concat_axis=0, tiled=True)
            )
        received = jnp.concatenate(received_parts, axis=3) if chunks > 1 else received_parts[0]
        count_freq = received.shape[0]
        cosine_table, sine_table = inverse_tables(count_freq, NT)
        widened = received.astype(jnp.float32)
        real_sum = 0.0
        imag_sum = 0.0
        for f in range(count_freq):
            real_sum = real_sum + widened[f, 0][:, None, :] * cosine_table[f][None, :, None]
            imag_sum = imag_sum + widened[f, 1][:, None, :] * sine_table[f][None, :, None]
        traces = (real_sum - imag_sum) * (1.0 / math.sqrt(count_freq))
        time_index = jnp.arange(NT, dtype=jnp.int32)[None, :, None]
        inside = (time_index >= window_bounds[0][:, None, :]) & (
            time_index < window_bounds[1][:, None, :]
        )
        return jnp.where(inside, traces, jnp.float32(0.0))

    return per_device


def solution(mesh):
    return jax.shard_map(
        make_per_device(mesh.shape["tile"]),
        mesh=mesh,
        in_specs=(
            P("freq", "grp", "tile", None),
            P("freq", "tile", None, "grp", None, None),
            P("freq", None, "grp", None, "tile"),
            P("freq", "grp", "tile"),
            P("grp", ("tile", "freq"), None),
        ),
        out_specs=P(("tile", "freq"), "grp", None),
        check_vma=False,
    )
```

```python
import math

import jax
import jax.numpy as jnp
from jax import lax
from jax.sharding import PartitionSpec as P

NT = 32
S_CHUNKS = 1


first_bin = 2


def inverse_tables(count_freq, count_time):
    freq_index = jnp.arange(count_freq, dtype=jnp.int32)[:, None] + first_bin
    time_index = jnp.arange(count_time, dtype=jnp.int32)[None, :]
    phase_step = freq_index * time_index % count_time
    angles = phase_step.astype(jnp.float32) * (2.0 * math.pi / count_time)
    return (jnp.cos(angles), jnp.sin(angles))


def column_products(v_local, x_local, rank_local):
    products = lax.dot_general(
        v_local, x_local, (((3,), (1,)), ((), ())), preferred_element_type=jnp.float32
    )
    coef_real = products[:, 0, :, 0] - products[:, 1, :, 1]
    coef_imag = products[:, 0, :, 1] + products[:, 1, :, 0]
    slot_index = jnp.arange(v_local.shape[2], dtype=jnp.int32)
    live_slots = slot_index[None, :, None] < rank_local[:, None, None]
    coef_real = jnp.where(live_slots, coef_real, jnp.float32(0.0)).astype(jnp.bfloat16)
    coef_imag = jnp.where(live_slots, coef_imag, jnp.float32(0.0)).astype(jnp.bfloat16)
    return jnp.stack([coef_real, coef_imag], axis=1)


def row_spectrum(u_local, blocks):
    products = lax.dot_general(
        u_local, blocks, (((0, 2), (0, 2)), ((), ())), preferred_element_type=jnp.float32
    )
    real_part = products[0, :, 0] - products[1, :, 1]
    imag_part = products[0, :, 1] + products[1, :, 0]
    return jnp.stack([real_part, imag_part], axis=0).astype(jnp.bfloat16)


def relay_exchange(own, u_local):
    t = lax.axis_index("tile")
    row = t // 2
    mine = lax.dynamic_index_in_dim(own, row, 0, keepdims=False)
    other = lax.dynamic_index_in_dim(own, 1 - row, 0, keepdims=False)
    across = lax.ppermute(other, "tile", [(0, 2), (2, 0), (1, 3), (3, 1)])
    swapped = lax.ppermute(
        jnp.stack([mine, across], axis=0), "tile", [(0, 1), (1, 0), (2, 3), (3, 2)]
    )
    columns = (t, t ^ 2, t ^ 1, t ^ 3)
    u_order = jnp.stack(
        [lax.dynamic_index_in_dim(u_local, j, 0, keepdims=False) for j in columns], axis=0
    )
    blocks = jnp.concatenate([mine[None], across[None], swapped], axis=0)
    return row_spectrum(u_order, blocks)


def gather_exchange(own, u_local, n_tile):
    repeat = n_tile // own.shape[0]
    sending = jnp.repeat(own, repeat, axis=0)
    received = lax.all_to_all(sending, "tile", split_axis=0, concat_axis=0, tiled=True)
    return row_spectrum(u_local, received)


def make_per_device(n_tile):
    def per_device(sources, v_factors, u_factors, tile_ranks, window_bounds):
        v_local = v_factors[0, 0]
        u_local = u_factors[0]
        x_local = sources[0]
        rank_local = tile_ranks[0, :, 0]
        rows = v_local.shape[0]
        use_relay = n_tile == 4 and rows == 2 and u_local.shape[0] == 4
        count_s = x_local.shape[2]
        chunks = S_CHUNKS if count_s % S_CHUNKS == 0 else 1
        width = count_s // chunks
        received_parts = []
        for c in range(chunks):
            x_part = x_local[:, :, c * width:(c + 1) * width]
            own = column_products(v_local, x_part, rank_local)
            if use_relay:
                spectrum = relay_exchange(own, u_local)
            else:
                spectrum = gather_exchange(own, u_local, n_tile)
            received_parts.append(
                lax.all_to_all(spectrum[None], "freq", split_axis=2, concat_axis=0, tiled=True)
            )
        received = jnp.concatenate(received_parts, axis=3) if chunks > 1 else received_parts[0]
        count_freq = received.shape[0]
        cosine_table, sine_table = inverse_tables(count_freq, NT)
        widened = received.astype(jnp.float32)
        real_sum = 0.0
        imag_sum = 0.0
        for f in range(count_freq):
            real_sum = real_sum + widened[f, 0][:, None, :] * cosine_table[f][None, :, None]
            imag_sum = imag_sum + widened[f, 1][:, None, :] * sine_table[f][None, :, None]
        traces = (real_sum - imag_sum) * (1.0 / math.sqrt(count_freq))
        time_index = jnp.arange(NT, dtype=jnp.int32)[None, :, None]
        inside = (time_index >= window_bounds[0][:, None, :]) & (
            time_index < window_bounds[1][:, None, :]
        )
        return jnp.where(inside, traces, jnp.float32(0.0))

    return per_device


def solution(mesh):
    return jax.shard_map(
        make_per_device(mesh.shape["tile"]),
        mesh=mesh,
        in_specs=(
            P("freq", "grp", "tile", None),
            P("freq", "tile", None, "grp", None, None),
            P("freq", None, "grp", None, "tile"),
            P("freq", "grp", "tile"),
            P("grp", ("tile", "freq"), None),
        ),
        out_specs=P(("tile", "freq"), "grp", None),
        check_vma=False,
    )
```

```python
import math

import jax
import jax.numpy as jnp
from jax import lax
from jax.sharding import PartitionSpec as P

NT = 32
S_CHUNKS = 1


first_bin = 2


def inverse_tables(count_freq, count_time):
    freq_index = jnp.arange(count_freq, dtype=jnp.int32)[:, None] + first_bin
    time_index = jnp.arange(count_time, dtype=jnp.int32)[None, :]
    phase_step = freq_index * time_index % count_time
    angles = phase_step.astype(jnp.float32) * (2.0 * math.pi / count_time)
    return (jnp.cos(angles), jnp.sin(angles))


def column_products(v_local, x_local, rank_local):
    products = lax.dot_general(
        v_local, x_local, (((3,), (1,)), ((), ())), preferred_element_type=jnp.float32
    )
    coef_real = products[:, 0, :, 0] - products[:, 1, :, 1]
    coef_imag = products[:, 0, :, 1] + products[:, 1, :, 0]
    slot_index = jnp.arange(v_local.shape[2], dtype=jnp.int32)
    live_slots = slot_index[None, :, None] < rank_local[:, None, None]
    coef_real = jnp.where(live_slots, coef_real, jnp.float32(0.0)).astype(jnp.bfloat16)
    coef_imag = jnp.where(live_slots, coef_imag, jnp.float32(0.0)).astype(jnp.bfloat16)
    return jnp.stack([coef_real, coef_imag], axis=1)


def row_spectrum(u_local, blocks):
    products = lax.dot_general(
        u_local, blocks, (((0, 2), (0, 2)), ((), ())), preferred_element_type=jnp.float32
    )
    real_part = products[0, :, 0] - products[1, :, 1]
    imag_part = products[0, :, 1] + products[1, :, 0]
    return jnp.stack([real_part, imag_part], axis=0).astype(jnp.bfloat16)


def relay_exchange(own, u_local):
    t = lax.axis_index("tile")
    row = t // 2
    mine = lax.dynamic_index_in_dim(own, row, 0, keepdims=False)
    other = lax.dynamic_index_in_dim(own, 1 - row, 0, keepdims=False)
    pairs = [(0, 1), (1, 0), (2, 3), (3, 2)]
    across = lax.ppermute(other, "tile", [(0, 2), (2, 0), (1, 3), (3, 1)])
    partner = lax.ppermute(mine, "tile", pairs)
    passed = lax.ppermute(across, "tile", pairs)
    columns = (t, t ^ 2, t ^ 1, t ^ 3)
    u_order = jnp.stack(
        [lax.dynamic_index_in_dim(u_local, j, 0, keepdims=False) for j in columns], axis=0
    )
    blocks = jnp.stack([mine, across, partner, passed], axis=0)
    return row_spectrum(u_order, blocks)


def gather_exchange(own, u_local, n_tile):
    repeat = n_tile // own.shape[0]
    sending = jnp.repeat(own, repeat, axis=0)
    received = lax.all_to_all(sending, "tile", split_axis=0, concat_axis=0, tiled=True)
    return row_spectrum(u_local, received)


def make_per_device(n_tile):
    def per_device(sources, v_factors, u_factors, tile_ranks, window_bounds):
        v_local = v_factors[0, 0]
        u_local = u_factors[0]
        x_local = sources[0]
        rank_local = tile_ranks[0, :, 0]
        rows = v_local.shape[0]
        use_relay = n_tile == 4 and rows == 2 and u_local.shape[0] == 4
        count_s = x_local.shape[2]
        chunks = S_CHUNKS if count_s % S_CHUNKS == 0 else 1
        width = count_s // chunks
        received_parts = []
        for c in range(chunks):
            x_part = x_local[:, :, c * width:(c + 1) * width]
            own = column_products(v_local, x_part, rank_local)
            if use_relay:
                spectrum = relay_exchange(own, u_local)
            else:
                spectrum = gather_exchange(own, u_local, n_tile)
            received_parts.append(
                lax.all_to_all(spectrum[None], "freq", split_axis=2, concat_axis=0, tiled=True)
            )
        received = jnp.concatenate(received_parts, axis=3) if chunks > 1 else received_parts[0]
        count_freq = received.shape[0]
        cosine_table, sine_table = inverse_tables(count_freq, NT)
        widened = received.astype(jnp.float32)
        real_sum = 0.0
        imag_sum = 0.0
        for f in range(count_freq):
            real_sum = real_sum + widened[f, 0][:, None, :] * cosine_table[f][None, :, None]
            imag_sum = imag_sum + widened[f, 1][:, None, :] * sine_table[f][None, :, None]
        traces = (real_sum - imag_sum) * (1.0 / math.sqrt(count_freq))
        time_index = jnp.arange(NT, dtype=jnp.int32)[None, :, None]
        inside = (time_index >= window_bounds[0][:, None, :]) & (
            time_index < window_bounds[1][:, None, :]
        )
        return jnp.where(inside, traces, jnp.float32(0.0))

    return per_device


def solution(mesh):
    return jax.shard_map(
        make_per_device(mesh.shape["tile"]),
        mesh=mesh,
        in_specs=(
            P("freq", "grp", "tile", None),
            P("freq", "tile", None, "grp", None, None),
            P("freq", None, "grp", None, "tile"),
            P("freq", "grp", "tile"),
            P("grp", ("tile", "freq"), None),
        ),
        out_specs=P(("tile", "freq"), "grp", None),
        check_vma=False,
    )
```

```python
import math

import jax
import jax.numpy as jnp
from jax import lax
from jax.sharding import PartitionSpec as P

NT = 32
S_CHUNKS = 2


first_bin = 2


def inverse_tables(count_freq, count_time):
    freq_index = jnp.arange(count_freq, dtype=jnp.int32)[:, None] + first_bin
    time_index = jnp.arange(count_time, dtype=jnp.int32)[None, :]
    phase_step = freq_index * time_index % count_time
    angles = phase_step.astype(jnp.float32) * (2.0 * math.pi / count_time)
    return (jnp.cos(angles), jnp.sin(angles))


def column_products(v_local, x_local, rank_local):
    products = lax.dot_general(
        v_local, x_local, (((3,), (1,)), ((), ())), preferred_element_type=jnp.float32
    )
    coef_real = products[:, 0, :, 0] - products[:, 1, :, 1]
    coef_imag = products[:, 0, :, 1] + products[:, 1, :, 0]
    slot_index = jnp.arange(v_local.shape[2], dtype=jnp.int32)
    live_slots = slot_index[None, :, None] < rank_local[:, None, None]
    coef_real = jnp.where(live_slots, coef_real, jnp.float32(0.0)).astype(jnp.bfloat16)
    coef_imag = jnp.where(live_slots, coef_imag, jnp.float32(0.0)).astype(jnp.bfloat16)
    return jnp.stack([coef_real, coef_imag], axis=1)


def row_spectrum(u_local, blocks):
    products = lax.dot_general(
        u_local, blocks, (((0, 2), (0, 2)), ((), ())), preferred_element_type=jnp.float32
    )
    real_part = products[0, :, 0] - products[1, :, 1]
    imag_part = products[0, :, 1] + products[1, :, 0]
    return jnp.stack([real_part, imag_part], axis=0).astype(jnp.bfloat16)


def relay_exchange(own, u_local):
    t = lax.axis_index("tile")
    row = t // 2
    mine = lax.dynamic_index_in_dim(own, row, 0, keepdims=False)
    other = lax.dynamic_index_in_dim(own, 1 - row, 0, keepdims=False)
    pairs = [(0, 1), (1, 0), (2, 3), (3, 2)]
    across = lax.ppermute(other, "tile", [(0, 2), (2, 0), (1, 3), (3, 1)])
    partner = lax.ppermute(mine, "tile", pairs)
    passed = lax.ppermute(across, "tile", pairs)
    columns = (t, t ^ 2, t ^ 1, t ^ 3)
    u_order = jnp.stack(
        [lax.dynamic_index_in_dim(u_local, j, 0, keepdims=False) for j in columns], axis=0
    )
    blocks = jnp.stack([mine, across, partner, passed], axis=0)
    return row_spectrum(u_order, blocks)


def gather_exchange(own, u_local, n_tile):
    repeat = n_tile // own.shape[0]
    sending = jnp.repeat(own, repeat, axis=0)
    received = lax.all_to_all(sending, "tile", split_axis=0, concat_axis=0, tiled=True)
    return row_spectrum(u_local, received)


def make_per_device(n_tile):
    def per_device(sources, v_factors, u_factors, tile_ranks, window_bounds):
        v_local = v_factors[0, 0]
        u_local = u_factors[0]
        x_local = sources[0]
        rank_local = tile_ranks[0, :, 0]
        rows = v_local.shape[0]
        use_relay = n_tile == 4 and rows == 2 and u_local.shape[0] == 4
        count_s = x_local.shape[2]
        chunks = S_CHUNKS if count_s % S_CHUNKS == 0 else 1
        width = count_s // chunks
        received_parts = []
        for c in range(chunks):
            x_part = x_local[:, :, c * width:(c + 1) * width]
            own = column_products(v_local, x_part, rank_local)
            if use_relay:
                spectrum = relay_exchange(own, u_local)
            else:
                spectrum = gather_exchange(own, u_local, n_tile)
            received_parts.append(
                lax.all_to_all(spectrum[None], "freq", split_axis=2, concat_axis=0, tiled=True)
            )
        received = jnp.concatenate(received_parts, axis=3) if chunks > 1 else received_parts[0]
        count_freq = received.shape[0]
        cosine_table, sine_table = inverse_tables(count_freq, NT)
        widened = received.astype(jnp.float32)
        real_sum = 0.0
        imag_sum = 0.0
        for f in range(count_freq):
            real_sum = real_sum + widened[f, 0][:, None, :] * cosine_table[f][None, :, None]
            imag_sum = imag_sum + widened[f, 1][:, None, :] * sine_table[f][None, :, None]
        traces = (real_sum - imag_sum) * (1.0 / math.sqrt(count_freq))
        time_index = jnp.arange(NT, dtype=jnp.int32)[None, :, None]
        inside = (time_index >= window_bounds[0][:, None, :]) & (
            time_index < window_bounds[1][:, None, :]
        )
        return jnp.where(inside, traces, jnp.float32(0.0))

    return per_device


def solution(mesh):
    return jax.shard_map(
        make_per_device(mesh.shape["tile"]),
        mesh=mesh,
        in_specs=(
            P("freq", "grp", "tile", None),
            P("freq", "tile", None, "grp", None, None),
            P("freq", None, "grp", None, "tile"),
            P("freq", "grp", "tile"),
            P("grp", ("tile", "freq"), None),
        ),
        out_specs=P(("tile", "freq"), "grp", None),
        check_vma=False,
    )
```

```python
import math

import jax
import jax.numpy as jnp
from jax import lax
from jax.sharding import PartitionSpec as P

NT = 32
S_CHUNKS = 1


first_bin = 2


def inverse_tables(count_freq, count_time):
    freq_index = jnp.arange(count_freq, dtype=jnp.int32)[:, None] + first_bin
    time_index = jnp.arange(count_time, dtype=jnp.int32)[None, :]
    phase_step = freq_index * time_index % count_time
    angles = phase_step.astype(jnp.float32) * (2.0 * math.pi / count_time)
    return (jnp.cos(angles), jnp.sin(angles))


def column_products(v_local, x_local, rank_local):
    products = lax.dot_general(
        v_local, x_local, (((3,), (1,)), ((), ())), preferred_element_type=jnp.float32
    )
    coef_real = products[:, 0, :, 0] - products[:, 1, :, 1]
    coef_imag = products[:, 0, :, 1] + products[:, 1, :, 0]
    slot_index = jnp.arange(v_local.shape[2], dtype=jnp.int32)
    live_slots = slot_index[None, :, None] < rank_local[:, None, None]
    coef_real = jnp.where(live_slots, coef_real, jnp.float32(0.0)).astype(jnp.bfloat16)
    coef_imag = jnp.where(live_slots, coef_imag, jnp.float32(0.0)).astype(jnp.bfloat16)
    return jnp.stack([coef_real, coef_imag], axis=1)


def row_spectrum(u_local, blocks):
    products = lax.dot_general(
        u_local, blocks, (((0, 2), (0, 2)), ((), ())), preferred_element_type=jnp.float32
    )
    real_part = products[0, :, 0] - products[1, :, 1]
    imag_part = products[0, :, 1] + products[1, :, 0]
    return jnp.stack([real_part, imag_part], axis=0).astype(jnp.bfloat16)


def relay_exchange(own, u_local):
    t = lax.axis_index("tile")
    row = t // 2
    mine = lax.dynamic_index_in_dim(own, row, 0, keepdims=False)
    other = lax.dynamic_index_in_dim(own, 1 - row, 0, keepdims=False)
    pairs = [(0, 1), (1, 0), (2, 3), (3, 2)]
    across = lax.ppermute(other, "tile", [(0, 2), (2, 0), (1, 3), (3, 1)])
    partner = lax.ppermute(mine, "tile", pairs)
    passed = lax.ppermute(across, "tile", pairs)
    columns = (t, t ^ 2, t ^ 1, t ^ 3)
    u_order = jnp.stack(
        [lax.dynamic_index_in_dim(u_local, j, 0, keepdims=False) for j in columns], axis=0
    )
    blocks = jnp.stack([mine, across, partner, passed], axis=0)
    return row_spectrum(u_order, blocks)


def gather_exchange(own, u_local, n_tile):
    repeat = n_tile // own.shape[0]
    sending = jnp.repeat(own, repeat, axis=0)
    received = lax.all_to_all(sending, "tile", split_axis=0, concat_axis=0, tiled=True)
    return row_spectrum(u_local, received)


def freq_exchange(spectrum, n_freq):
    f = lax.axis_index("freq")
    width = spectrum.shape[1] // n_freq
    pieces = [(f, lax.dynamic_slice_in_dim(spectrum, f * width, width, axis=1))]
    for d in range(1, n_freq):
        part = lax.dynamic_slice_in_dim(spectrum, (f ^ d) * width, width, axis=1)
        pairs = [(i, i ^ d) for i in range(n_freq)]
        pieces.append((f ^ d, lax.ppermute(part, "freq", pairs)))
    return pieces


def make_per_device(n_tile, n_freq):
    def per_device(sources, v_factors, u_factors, tile_ranks, window_bounds):
        v_local = v_factors[0, 0]
        u_local = u_factors[0]
        x_local = sources[0]
        rank_local = tile_ranks[0, :, 0]
        rows = v_local.shape[0]
        use_relay = n_tile == 4 and rows == 2 and u_local.shape[0] == 4
        use_swaps = n_freq & (n_freq - 1) == 0
        count_s = x_local.shape[2]
        chunks = S_CHUNKS if count_s % S_CHUNKS == 0 else 1
        width = count_s // chunks
        received_parts = []
        for c in range(chunks):
            x_part = x_local[:, :, c * width:(c + 1) * width]
            own = column_products(v_local, x_part, rank_local)
            if use_relay:
                spectrum = relay_exchange(own, u_local)
            else:
                spectrum = gather_exchange(own, u_local, n_tile)
            if use_swaps:
                received_parts.append(freq_exchange(spectrum, n_freq))
            else:
                received = lax.all_to_all(
                    spectrum[None], "freq", split_axis=2, concat_axis=0, tiled=True
                )
                received_parts.append([(f, received[f]) for f in range(n_freq)])
        pieces = [
            (
                index,
                jnp.concatenate([part[k][1] for part in received_parts], axis=2)
                if chunks > 1
                else piece,
            )
            for k, (index, piece) in enumerate(received_parts[0])
        ]
        cosine_table, sine_table = inverse_tables(n_freq, NT)
        scale = 1.0 / math.sqrt(n_freq)
        traces = 0.0
        for index, piece in pieces:
            cosine = lax.dynamic_index_in_dim(cosine_table, index, 0, keepdims=False) * scale
            sine = lax.dynamic_index_in_dim(sine_table, index, 0, keepdims=False) * scale
            widened = piece.astype(jnp.float32)
            traces = (
                traces
                + widened[0][:, None, :] * cosine[None, :, None]
                - widened[1][:, None, :] * sine[None, :, None]
            )
        time_index = jnp.arange(NT, dtype=jnp.int32)[None, :, None]
        inside = (time_index >= window_bounds[0][:, None, :]) & (
            time_index < window_bounds[1][:, None, :]
        )
        return jnp.where(inside, traces, jnp.float32(0.0))

    return per_device


def solution(mesh):
    return jax.shard_map(
        make_per_device(mesh.shape["tile"], mesh.shape["freq"]),
        mesh=mesh,
        in_specs=(
            P("freq", "grp", "tile", None),
            P("freq", "tile", None, "grp", None, None),
            P("freq", None, "grp", None, "tile"),
            P("freq", "grp", "tile"),
            P("grp", ("tile", "freq"), None),
        ),
        out_specs=P(("tile", "freq"), "grp", None),
        check_vma=False,
    )
```

```python
import math

import jax
import jax.numpy as jnp
from jax import lax
from jax.sharding import PartitionSpec as P

NT = 32
S_CHUNKS = 2


first_bin = 2


def inverse_tables(count_freq, count_time):
    freq_index = jnp.arange(count_freq, dtype=jnp.int32)[:, None] + first_bin
    time_index = jnp.arange(count_time, dtype=jnp.int32)[None, :]
    phase_step = freq_index * time_index % count_time
    angles = phase_step.astype(jnp.float32) * (2.0 * math.pi / count_time)
    return (jnp.cos(angles), jnp.sin(angles))


def column_products(v_local, x_local, rank_local):
    products = lax.dot_general(
        v_local, x_local, (((3,), (1,)), ((), ())), preferred_element_type=jnp.float32
    )
    coef_real = products[:, 0, :, 0] - products[:, 1, :, 1]
    coef_imag = products[:, 0, :, 1] + products[:, 1, :, 0]
    slot_index = jnp.arange(v_local.shape[2], dtype=jnp.int32)
    live_slots = slot_index[None, :, None] < rank_local[:, None, None]
    coef_real = jnp.where(live_slots, coef_real, jnp.float32(0.0)).astype(jnp.bfloat16)
    coef_imag = jnp.where(live_slots, coef_imag, jnp.float32(0.0)).astype(jnp.bfloat16)
    return jnp.stack([coef_real, coef_imag], axis=1)


def row_spectrum(u_local, blocks):
    products = lax.dot_general(
        u_local, blocks, (((0, 2), (0, 2)), ((), ())), preferred_element_type=jnp.float32
    )
    real_part = products[0, :, 0] - products[1, :, 1]
    imag_part = products[0, :, 1] + products[1, :, 0]
    return jnp.stack([real_part, imag_part], axis=0).astype(jnp.bfloat16)


def relay_exchange(own, u_local):
    t = lax.axis_index("tile")
    row = t // 2
    mine = lax.dynamic_index_in_dim(own, row, 0, keepdims=False)
    other = lax.dynamic_index_in_dim(own, 1 - row, 0, keepdims=False)
    pairs = [(0, 1), (1, 0), (2, 3), (3, 2)]
    across = lax.ppermute(other, "tile", [(0, 2), (2, 0), (1, 3), (3, 1)])
    partner = lax.ppermute(mine, "tile", pairs)
    passed = lax.ppermute(across, "tile", pairs)
    columns = (t, t ^ 2, t ^ 1, t ^ 3)
    u_order = jnp.stack(
        [lax.dynamic_index_in_dim(u_local, j, 0, keepdims=False) for j in columns], axis=0
    )
    blocks = jnp.stack([mine, across, partner, passed], axis=0)
    return row_spectrum(u_order, blocks)


def gather_exchange(own, u_local, n_tile):
    repeat = n_tile // own.shape[0]
    sending = jnp.repeat(own, repeat, axis=0)
    received = lax.all_to_all(sending, "tile", split_axis=0, concat_axis=0, tiled=True)
    return row_spectrum(u_local, received)


def freq_exchange(spectrum, n_freq):
    f = lax.axis_index("freq")
    width = spectrum.shape[1] // n_freq
    pieces = [(f, lax.dynamic_slice_in_dim(spectrum, f * width, width, axis=1))]
    for d in range(1, n_freq):
        part = lax.dynamic_slice_in_dim(spectrum, (f ^ d) * width, width, axis=1)
        pairs = [(i, i ^ d) for i in range(n_freq)]
        pieces.append((f ^ d, lax.ppermute(part, "freq", pairs)))
    return pieces


def make_per_device(n_tile, n_freq):
    def per_device(sources, v_factors, u_factors, tile_ranks, window_bounds):
        v_local = v_factors[0, 0]
        u_local = u_factors[0]
        x_local = sources[0]
        rank_local = tile_ranks[0, :, 0]
        rows = v_local.shape[0]
        use_relay = n_tile == 4 and rows == 2 and u_local.shape[0] == 4
        use_swaps = n_freq & (n_freq - 1) == 0
        count_s = x_local.shape[2]
        chunks = S_CHUNKS if count_s % S_CHUNKS == 0 else 1
        width = count_s // chunks
        received_parts = []
        for c in range(chunks):
            x_part = x_local[:, :, c * width:(c + 1) * width]
            own = column_products(v_local, x_part, rank_local)
            if use_relay:
                spectrum = relay_exchange(own, u_local)
            else:
                spectrum = gather_exchange(own, u_local, n_tile)
            if use_swaps:
                received_parts.append(freq_exchange(spectrum, n_freq))
            else:
                received = lax.all_to_all(
                    spectrum[None], "freq", split_axis=2, concat_axis=0, tiled=True
                )
                received_parts.append([(f, received[f]) for f in range(n_freq)])
        pieces = [
            (
                index,
                jnp.concatenate([part[k][1] for part in received_parts], axis=2)
                if chunks > 1
                else piece,
            )
            for k, (index, piece) in enumerate(received_parts[0])
        ]
        cosine_table, sine_table = inverse_tables(n_freq, NT)
        scale = 1.0 / math.sqrt(n_freq)
        traces = 0.0
        for index, piece in pieces:
            cosine = lax.dynamic_index_in_dim(cosine_table, index, 0, keepdims=False) * scale
            sine = lax.dynamic_index_in_dim(sine_table, index, 0, keepdims=False) * scale
            widened = piece.astype(jnp.float32)
            traces = (
                traces
                + widened[0][:, None, :] * cosine[None, :, None]
                - widened[1][:, None, :] * sine[None, :, None]
            )
        time_index = jnp.arange(NT, dtype=jnp.int32)[None, :, None]
        inside = (time_index >= window_bounds[0][:, None, :]) & (
            time_index < window_bounds[1][:, None, :]
        )
        return jnp.where(inside, traces, jnp.float32(0.0))

    return per_device


def solution(mesh):
    return jax.shard_map(
        make_per_device(mesh.shape["tile"], mesh.shape["freq"]),
        mesh=mesh,
        in_specs=(
            P("freq", "grp", "tile", None),
            P("freq", "tile", None, "grp", None, None),
            P("freq", None, "grp", None, "tile"),
            P("freq", "grp", "tile"),
            P("grp", ("tile", "freq"), None),
        ),
        out_specs=P(("tile", "freq"), "grp", None),
        check_vma=False,
    )
```

```python
import math

import jax
import jax.numpy as jnp
from jax import lax
from jax.experimental import pallas as pl
from jax.sharding import PartitionSpec as P

NT = 32
S_CHUNKS = 1


first_bin = 2


def inverse_tables(count_freq, count_time):
    freq_index = jnp.arange(count_freq, dtype=jnp.int32)[:, None] + first_bin
    time_index = jnp.arange(count_time, dtype=jnp.int32)[None, :]
    phase_step = freq_index * time_index % count_time
    angles = phase_step.astype(jnp.float32) * (2.0 * math.pi / count_time)
    return (jnp.cos(angles), jnp.sin(angles))


def column_products(v_local, x_local, rank_local):
    products = lax.dot_general(
        v_local, x_local, (((3,), (1,)), ((), ())), preferred_element_type=jnp.float32
    )
    coef_real = products[:, 0, :, 0] - products[:, 1, :, 1]
    coef_imag = products[:, 0, :, 1] + products[:, 1, :, 0]
    slot_index = jnp.arange(v_local.shape[2], dtype=jnp.int32)
    live_slots = slot_index[None, :, None] < rank_local[:, None, None]
    coef_real = jnp.where(live_slots, coef_real, jnp.float32(0.0)).astype(jnp.bfloat16)
    coef_imag = jnp.where(live_slots, coef_imag, jnp.float32(0.0)).astype(jnp.bfloat16)
    return jnp.stack([coef_real, coef_imag], axis=1)


def row_spectrum(u_local, blocks):
    products = lax.dot_general(
        u_local, blocks, (((0, 2), (0, 2)), ((), ())), preferred_element_type=jnp.float32
    )
    real_part = products[0, :, 0] - products[1, :, 1]
    imag_part = products[0, :, 1] + products[1, :, 0]
    return jnp.stack([real_part, imag_part], axis=0).astype(jnp.bfloat16)


def relay_exchange(own, u_local):
    t = lax.axis_index("tile")
    row = t // 2
    mine = lax.dynamic_index_in_dim(own, row, 0, keepdims=False)
    other = lax.dynamic_index_in_dim(own, 1 - row, 0, keepdims=False)
    pairs = [(0, 1), (1, 0), (2, 3), (3, 2)]
    across = lax.ppermute(other, "tile", [(0, 2), (2, 0), (1, 3), (3, 1)])
    partner = lax.ppermute(mine, "tile", pairs)
    passed = lax.ppermute(across, "tile", pairs)
    columns = (t, t ^ 2, t ^ 1, t ^ 3)
    u_order = jnp.stack(
        [lax.dynamic_index_in_dim(u_local, j, 0, keepdims=False) for j in columns], axis=0
    )
    blocks = jnp.stack([mine, across, partner, passed], axis=0)
    return row_spectrum(u_order, blocks)


def gather_exchange(own, u_local, n_tile):
    repeat = n_tile // own.shape[0]
    sending = jnp.repeat(own, repeat, axis=0)
    received = lax.all_to_all(sending, "tile", split_axis=0, concat_axis=0, tiled=True)
    return row_spectrum(u_local, received)


def freq_exchange(spectrum, n_freq):
    f = lax.axis_index("freq")
    width = spectrum.shape[1] // n_freq
    pieces = [(f, lax.dynamic_slice_in_dim(spectrum, f * width, width, axis=1))]
    for d in range(1, n_freq):
        part = lax.dynamic_slice_in_dim(spectrum, (f ^ d) * width, width, axis=1)
        pairs = [(i, i ^ d) for i in range(n_freq)]
        pieces.append((f ^ d, lax.ppermute(part, "freq", pairs)))
    return pieces


def traces_kernel(table_ref, *refs):
    piece_refs = refs[:-2]
    bounds_ref, out_ref = refs[-2], refs[-1]
    half = table_ref.shape[1]
    count = len(piece_refs)
    time_index = lax.broadcasted_iota(jnp.int32, (half, table_ref.shape[2]), 0)
    for i in range(out_ref.shape[0]):
        sums = [None, None]
        for k, piece_ref in enumerate(piece_refs):
            real = piece_ref[0, i:i + 1, :]
            imag = piece_ref[1, i:i + 1, :]
            term = real * table_ref[2 * k] - imag * table_ref[2 * k + 1]
            sums[k % 2] = term if sums[k % 2] is None else sums[k % 2] + term
        even = sums[0]
        odd = sums[1] if sums[1] is not None else jnp.zeros_like(even)
        first = bounds_ref[0, i:i + 1, :]
        last = bounds_ref[1, i:i + 1, :]
        low = even + odd
        out_ref[i, 0:half, :] = jnp.where(
            (time_index >= first) & (time_index < last), low, jnp.float32(0.0)
        )
        high = (even - odd) * table_ref[2 * count]
        later = time_index + half
        out_ref[i, half:2 * half, :] = jnp.where(
            (later >= first) & (later < last), high, jnp.float32(0.0)
        )


def windowed_traces(pieces, window_bounds, n_freq):
    cosine_table, sine_table = inverse_tables(n_freq, NT)
    scale = 1.0 / math.sqrt(n_freq)
    half = NT // 2
    count_m, count_s = window_bounds.shape[1], window_bounds.shape[2]
    rows = []
    for index, _ in pieces:
        for table in (cosine_table, sine_table):
            row = lax.dynamic_index_in_dim(table, index, 0, keepdims=False)[:half] * scale
            rows.append(jnp.broadcast_to(row[:, None], (half, count_s)))
    parity = (pieces[0][0] + first_bin) % 2
    sign = jnp.asarray(1 - 2 * parity, jnp.float32)
    rows.append(jnp.full((half, count_s), sign, jnp.float32))
    table = jnp.stack(rows, axis=0)
    block_m = 8 if count_m % 8 == 0 else count_m
    piece_spec = pl.BlockSpec((2, block_m, count_s), lambda g: (0, g, 0))
    return pl.pallas_call(
        traces_kernel,
        grid=(count_m // block_m,),
        in_specs=[pl.BlockSpec(table.shape, lambda g: (0, 0, 0))]
        + [piece_spec] * len(pieces)
        + [piece_spec],
        out_specs=pl.BlockSpec((block_m, NT, count_s), lambda g: (g, 0, 0)),
        out_shape=jax.ShapeDtypeStruct((count_m, NT, count_s), jnp.float32),
    )(table, *[piece.astype(jnp.float32) for _, piece in pieces], window_bounds)


def make_per_device(n_tile, n_freq):
    def per_device(sources, v_factors, u_factors, tile_ranks, window_bounds):
        v_local = v_factors[0, 0]
        u_local = u_factors[0]
        x_local = sources[0]
        rank_local = tile_ranks[0, :, 0]
        rows = v_local.shape[0]
        use_relay = n_tile == 4 and rows == 2 and u_local.shape[0] == 4
        use_swaps = n_freq & (n_freq - 1) == 0
        count_s = x_local.shape[2]
        chunks = S_CHUNKS if count_s % S_CHUNKS == 0 else 1
        width = count_s // chunks
        received_parts = []
        for c in range(chunks):
            x_part = x_local[:, :, c * width:(c + 1) * width]
            own = column_products(v_local, x_part, rank_local)
            if use_relay:
                spectrum = relay_exchange(own, u_local)
            else:
                spectrum = gather_exchange(own, u_local, n_tile)
            if use_swaps:
                received_parts.append(freq_exchange(spectrum, n_freq))
            else:
                received = lax.all_to_all(
                    spectrum[None], "freq", split_axis=2, concat_axis=0, tiled=True
                )
                received_parts.append([(f, received[f]) for f in range(n_freq)])
        pieces = [
            (
                index,
                jnp.concatenate([part[k][1] for part in received_parts], axis=2)
                if chunks > 1
                else piece,
            )
            for k, (index, piece) in enumerate(received_parts[0])
        ]
        return windowed_traces(pieces, window_bounds, n_freq)

    return per_device


def solution(mesh):
    return jax.shard_map(
        make_per_device(mesh.shape["tile"], mesh.shape["freq"]),
        mesh=mesh,
        in_specs=(
            P("freq", "grp", "tile", None),
            P("freq", "tile", None, "grp", None, None),
            P("freq", None, "grp", None, "tile"),
            P("freq", "grp", "tile"),
            P("grp", ("tile", "freq"), None),
        ),
        out_specs=P(("tile", "freq"), "grp", None),
        check_vma=False,
    )
```

```python
import math

import jax
import jax.numpy as jnp
from jax import lax
from jax.sharding import PartitionSpec as P

NT = 32
S_CHUNKS = 1


first_bin = 2


def inverse_tables(count_freq, count_time):
    freq_index = jnp.arange(count_freq, dtype=jnp.int32)[:, None] + first_bin
    time_index = jnp.arange(count_time, dtype=jnp.int32)[None, :]
    phase_step = freq_index * time_index % count_time
    angles = phase_step.astype(jnp.float32) * (2.0 * math.pi / count_time)
    return (jnp.cos(angles), jnp.sin(angles))


def column_products(v_local, x_local, rank_local):
    products = lax.dot_general(
        v_local, x_local, (((3,), (1,)), ((), ())), preferred_element_type=jnp.float32
    )
    coef_real = products[:, 0, :, 0] - products[:, 1, :, 1]
    coef_imag = products[:, 0, :, 1] + products[:, 1, :, 0]
    slot_index = jnp.arange(v_local.shape[2], dtype=jnp.int32)
    live_slots = slot_index[None, :, None] < rank_local[:, None, None]
    coef_real = jnp.where(live_slots, coef_real, jnp.float32(0.0)).astype(jnp.bfloat16)
    coef_imag = jnp.where(live_slots, coef_imag, jnp.float32(0.0)).astype(jnp.bfloat16)
    return jnp.stack([coef_real, coef_imag], axis=1)


def row_spectrum(u_local, blocks):
    products = lax.dot_general(
        u_local, blocks, (((0, 2), (0, 2)), ((), ())), preferred_element_type=jnp.float32
    )
    real_part = products[0, :, 0] - products[1, :, 1]
    imag_part = products[0, :, 1] + products[1, :, 0]
    return jnp.stack([real_part, imag_part], axis=0).astype(jnp.bfloat16)


def relay_exchange(own, u_local):
    t = lax.axis_index("tile")
    row = t // 2
    mine = lax.dynamic_index_in_dim(own, row, 0, keepdims=False)
    other = lax.dynamic_index_in_dim(own, 1 - row, 0, keepdims=False)
    pairs = [(0, 1), (1, 0), (2, 3), (3, 2)]
    across = lax.ppermute(other, "tile", [(0, 2), (2, 0), (1, 3), (3, 1)])
    partner = lax.ppermute(mine, "tile", pairs)
    passed = lax.ppermute(across, "tile", pairs)
    columns = (t, t ^ 2, t ^ 1, t ^ 3)
    u_order = jnp.stack(
        [lax.dynamic_index_in_dim(u_local, j, 0, keepdims=False) for j in columns], axis=0
    )
    blocks = jnp.stack([mine, across, partner, passed], axis=0)
    return row_spectrum(u_order, blocks)


def gather_exchange(own, u_local, n_tile):
    repeat = n_tile // own.shape[0]
    sending = jnp.repeat(own, repeat, axis=0)
    received = lax.all_to_all(sending, "tile", split_axis=0, concat_axis=0, tiled=True)
    return row_spectrum(u_local, received)


def freq_exchange(spectrum, n_freq):
    f = lax.axis_index("freq")
    width = spectrum.shape[1] // n_freq
    pieces = [(f, lax.dynamic_slice_in_dim(spectrum, f * width, width, axis=1))]
    for d in range(1, n_freq):
        part = lax.dynamic_slice_in_dim(spectrum, (f ^ d) * width, width, axis=1)
        pairs = [(i, i ^ d) for i in range(n_freq)]
        pieces.append((f ^ d, lax.ppermute(part, "freq", pairs)))
    return pieces


def make_per_device(n_tile, n_freq):
    def per_device(sources, v_factors, u_factors, tile_ranks, window_bounds):
        v_local = v_factors[0, 0]
        u_local = u_factors[0]
        x_local = sources[0]
        rank_local = tile_ranks[0, :, 0]
        rows = v_local.shape[0]
        use_relay = n_tile == 4 and rows == 2 and u_local.shape[0] == 4
        use_swaps = n_freq & (n_freq - 1) == 0
        count_s = x_local.shape[2]
        chunks = S_CHUNKS if count_s % S_CHUNKS == 0 else 1
        width = count_s // chunks
        received_parts = []
        for c in range(chunks):
            x_part = x_local[:, :, c * width:(c + 1) * width]
            own = column_products(v_local, x_part, rank_local)
            if use_relay:
                spectrum = relay_exchange(own, u_local)
            else:
                spectrum = gather_exchange(own, u_local, n_tile)
            if use_swaps:
                received_parts.append(freq_exchange(spectrum, n_freq))
            else:
                received = lax.all_to_all(
                    spectrum[None], "freq", split_axis=2, concat_axis=0, tiled=True
                )
                received_parts.append([(f, received[f]) for f in range(n_freq)])
        pieces = [
            (
                index,
                jnp.concatenate([part[k][1] for part in received_parts], axis=2)
                if chunks > 1
                else piece,
            )
            for k, (index, piece) in enumerate(received_parts[0])
        ]
        cosine_table, sine_table = inverse_tables(n_freq, NT)
        scale = 1.0 / math.sqrt(n_freq)
        count_s = window_bounds.shape[2]
        rows = []
        for index, _ in pieces:
            for table in (cosine_table, sine_table):
                row = lax.dynamic_index_in_dim(table, index, 0, keepdims=False) * scale
                rows.append(jnp.broadcast_to(row[:, None], (NT, count_s)))
        rows = lax.optimization_barrier(rows)
        traces = 0.0
        for k, (_, piece) in enumerate(pieces):
            widened = piece.astype(jnp.float32)
            traces = (
                traces
                + widened[0][:, None, :] * rows[2 * k][None]
                - widened[1][:, None, :] * rows[2 * k + 1][None]
            )
        time_index = jnp.arange(NT, dtype=jnp.int32)[None, :, None]
        inside = (time_index >= window_bounds[0][:, None, :]) & (
            time_index < window_bounds[1][:, None, :]
        )
        return jnp.where(inside, traces, jnp.float32(0.0))

    return per_device


def solution(mesh):
    return jax.shard_map(
        make_per_device(mesh.shape["tile"], mesh.shape["freq"]),
        mesh=mesh,
        in_specs=(
            P("freq", "grp", "tile", None),
            P("freq", "tile", None, "grp", None, None),
            P("freq", None, "grp", None, "tile"),
            P("freq", "grp", "tile"),
            P("grp", ("tile", "freq"), None),
        ),
        out_specs=P(("tile", "freq"), "grp", None),
        check_vma=False,
    )
```

```python
import math

import jax
import jax.numpy as jnp
from jax import lax
from jax.sharding import PartitionSpec as P

NT = 32
S_CHUNKS = 2


first_bin = 2


def inverse_tables(count_freq, count_time):
    freq_index = jnp.arange(count_freq, dtype=jnp.int32)[:, None] + first_bin
    time_index = jnp.arange(count_time, dtype=jnp.int32)[None, :]
    phase_step = freq_index * time_index % count_time
    angles = phase_step.astype(jnp.float32) * (2.0 * math.pi / count_time)
    return (jnp.cos(angles), jnp.sin(angles))


def column_products(v_local, x_local, rank_local):
    products = lax.dot_general(
        v_local, x_local, (((3,), (1,)), ((), ())), preferred_element_type=jnp.float32
    )
    coef_real = products[:, 0, :, 0] - products[:, 1, :, 1]
    coef_imag = products[:, 0, :, 1] + products[:, 1, :, 0]
    slot_index = jnp.arange(v_local.shape[2], dtype=jnp.int32)
    live_slots = slot_index[None, :, None] < rank_local[:, None, None]
    coef_real = jnp.where(live_slots, coef_real, jnp.float32(0.0)).astype(jnp.bfloat16)
    coef_imag = jnp.where(live_slots, coef_imag, jnp.float32(0.0)).astype(jnp.bfloat16)
    return jnp.stack([coef_real, coef_imag], axis=1)


def row_spectrum(u_local, blocks):
    products = lax.dot_general(
        u_local, blocks, (((0, 2), (0, 2)), ((), ())), preferred_element_type=jnp.float32
    )
    real_part = products[0, :, 0] - products[1, :, 1]
    imag_part = products[0, :, 1] + products[1, :, 0]
    return jnp.stack([real_part, imag_part], axis=0).astype(jnp.bfloat16)


def relay_exchange(own, u_local, after=None):
    t = lax.axis_index("tile")
    row = t // 2
    mine = lax.dynamic_index_in_dim(own, row, 0, keepdims=False)
    other = lax.dynamic_index_in_dim(own, 1 - row, 0, keepdims=False)
    if after is not None:
        mine, other, _ = lax.optimization_barrier((mine, other, after))
    pairs = [(0, 1), (1, 0), (2, 3), (3, 2)]
    across = lax.ppermute(other, "tile", [(0, 2), (2, 0), (1, 3), (3, 1)])
    partner = lax.ppermute(mine, "tile", pairs)
    passed = lax.ppermute(across, "tile", pairs)
    columns = (t, t ^ 2, t ^ 1, t ^ 3)
    u_order = jnp.stack(
        [lax.dynamic_index_in_dim(u_local, j, 0, keepdims=False) for j in columns], axis=0
    )
    blocks = jnp.stack([mine, across, partner, passed], axis=0)
    return row_spectrum(u_order, blocks), across


def gather_exchange(own, u_local, n_tile):
    repeat = n_tile // own.shape[0]
    sending = jnp.repeat(own, repeat, axis=0)
    received = lax.all_to_all(sending, "tile", split_axis=0, concat_axis=0, tiled=True)
    return row_spectrum(u_local, received)


def freq_exchange(spectrum, n_freq):
    f = lax.axis_index("freq")
    width = spectrum.shape[1] // n_freq
    pieces = [(f, lax.dynamic_slice_in_dim(spectrum, f * width, width, axis=1))]
    for d in range(1, n_freq):
        part = lax.dynamic_slice_in_dim(spectrum, (f ^ d) * width, width, axis=1)
        pairs = [(i, i ^ d) for i in range(n_freq)]
        pieces.append((f ^ d, lax.ppermute(part, "freq", pairs)))
    return pieces


def make_per_device(n_tile, n_freq):
    def per_device(sources, v_factors, u_factors, tile_ranks, window_bounds):
        v_local = v_factors[0, 0]
        u_local = u_factors[0]
        x_local = sources[0]
        rank_local = tile_ranks[0, :, 0]
        rows = v_local.shape[0]
        use_relay = n_tile == 4 and rows == 2 and u_local.shape[0] == 4
        use_swaps = n_freq & (n_freq - 1) == 0
        count_s = x_local.shape[2]
        chunks = S_CHUNKS if count_s % S_CHUNKS == 0 else 1
        width = count_s // chunks
        received_parts = []
        after = None
        for c in range(chunks):
            x_part = x_local[:, :, c * width:(c + 1) * width]
            own = column_products(v_local, x_part, rank_local)
            if use_relay:
                spectrum, after = relay_exchange(own, u_local, after)
            else:
                spectrum = gather_exchange(own, u_local, n_tile)
            if use_swaps:
                received_parts.append(freq_exchange(spectrum, n_freq))
            else:
                received = lax.all_to_all(
                    spectrum[None], "freq", split_axis=2, concat_axis=0, tiled=True
                )
                received_parts.append([(f, received[f]) for f in range(n_freq)])
        pieces = [
            (
                index,
                jnp.concatenate([part[k][1] for part in received_parts], axis=2)
                if chunks > 1
                else piece,
            )
            for k, (index, piece) in enumerate(received_parts[0])
        ]
        cosine_table, sine_table = inverse_tables(n_freq, NT)
        scale = 1.0 / math.sqrt(n_freq)
        count_s = window_bounds.shape[2]
        rows = []
        for index, _ in pieces:
            for table in (cosine_table, sine_table):
                row = lax.dynamic_index_in_dim(table, index, 0, keepdims=False) * scale
                rows.append(jnp.broadcast_to(row[:, None], (NT, count_s)))
        rows = lax.optimization_barrier(rows)
        traces = 0.0
        for k, (_, piece) in enumerate(pieces):
            widened = piece.astype(jnp.float32)
            traces = (
                traces
                + widened[0][:, None, :] * rows[2 * k][None]
                - widened[1][:, None, :] * rows[2 * k + 1][None]
            )
        time_index = jnp.arange(NT, dtype=jnp.int32)[None, :, None]
        inside = (time_index >= window_bounds[0][:, None, :]) & (
            time_index < window_bounds[1][:, None, :]
        )
        return jnp.where(inside, traces, jnp.float32(0.0))

    return per_device


def solution(mesh):
    return jax.shard_map(
        make_per_device(mesh.shape["tile"], mesh.shape["freq"]),
        mesh=mesh,
        in_specs=(
            P("freq", "grp", "tile", None),
            P("freq", "tile", None, "grp", None, None),
            P("freq", None, "grp", None, "tile"),
            P("freq", "grp", "tile"),
            P("grp", ("tile", "freq"), None),
        ),
        out_specs=P(("tile", "freq"), "grp", None),
        check_vma=False,
    )
```

```python
import math

import jax
import jax.numpy as jnp
from jax import lax
from jax.sharding import PartitionSpec as P

NT = 32
S_CHUNKS = 1


first_bin = 2


def inverse_tables(count_freq, count_time):
    freq_index = jnp.arange(count_freq, dtype=jnp.int32)[:, None] + first_bin
    time_index = jnp.arange(count_time, dtype=jnp.int32)[None, :]
    phase_step = freq_index * time_index % count_time
    angles = phase_step.astype(jnp.float32) * (2.0 * math.pi / count_time)
    return (jnp.cos(angles), jnp.sin(angles))


def column_products(v_local, x_local, rank_local):
    products = lax.dot_general(
        v_local, x_local, (((3,), (1,)), ((), ())), preferred_element_type=jnp.float32
    )
    coef_real = products[:, 0, :, 0] - products[:, 1, :, 1]
    coef_imag = products[:, 0, :, 1] + products[:, 1, :, 0]
    slot_index = jnp.arange(v_local.shape[2], dtype=jnp.int32)
    live_slots = slot_index[None, :, None] < rank_local[:, None, None]
    coef_real = jnp.where(live_slots, coef_real, jnp.float32(0.0)).astype(jnp.bfloat16)
    coef_imag = jnp.where(live_slots, coef_imag, jnp.float32(0.0)).astype(jnp.bfloat16)
    return jnp.stack([coef_real, coef_imag], axis=1)


def row_spectrum(u_local, blocks):
    products = lax.dot_general(
        u_local, blocks, (((0, 2), (0, 2)), ((), ())), preferred_element_type=jnp.float32
    )
    real_part = products[0, :, 0] - products[1, :, 1]
    imag_part = products[0, :, 1] + products[1, :, 0]
    return jnp.stack([real_part, imag_part], axis=0).astype(jnp.bfloat16)


def row_products(u_part, blocks):
    return lax.dot_general(
        u_part, blocks, (((0, 2), (0, 2)), ((), ())), preferred_element_type=jnp.float32
    )


def finish_spectrum(products):
    real_part = products[0, :, 0] - products[1, :, 1]
    imag_part = products[0, :, 1] + products[1, :, 0]
    return jnp.stack([real_part, imag_part], axis=0).astype(jnp.bfloat16)


def relay_exchange(v_local, x_local, rank_local, u_local):
    t = lax.axis_index("tile")
    row = t // 2

    def block_of(r):
        v_row = lax.dynamic_index_in_dim(v_local, r, 0, keepdims=True)
        rank_row = lax.dynamic_index_in_dim(rank_local, r, 0, keepdims=True)
        return column_products(v_row, x_local, rank_row)[0]

    pairs = [(0, 1), (1, 0), (2, 3), (3, 2)]
    across = lax.ppermute(block_of(1 - row), "tile", [(0, 2), (2, 0), (1, 3), (3, 1)])
    mine = block_of(row)
    partner = lax.ppermute(mine, "tile", pairs)
    passed = lax.ppermute(across, "tile", pairs)
    columns = (t, t ^ 2, t ^ 1, t ^ 3)
    u_order = [lax.dynamic_index_in_dim(u_local, j, 0, keepdims=False) for j in columns]
    early = row_products(jnp.stack(u_order[:3], axis=0), jnp.stack([mine, across, partner], axis=0))
    late = row_products(u_order[3][None], passed[None])
    return finish_spectrum(early + late)


def gather_exchange(own, u_local, n_tile):
    repeat = n_tile // own.shape[0]
    sending = jnp.repeat(own, repeat, axis=0)
    received = lax.all_to_all(sending, "tile", split_axis=0, concat_axis=0, tiled=True)
    return row_spectrum(u_local, received)


def freq_exchange(spectrum, n_freq):
    f = lax.axis_index("freq")
    width = spectrum.shape[1] // n_freq
    pieces = [(f, lax.dynamic_slice_in_dim(spectrum, f * width, width, axis=1))]
    for d in range(1, n_freq):
        part = lax.dynamic_slice_in_dim(spectrum, (f ^ d) * width, width, axis=1)
        pairs = [(i, i ^ d) for i in range(n_freq)]
        pieces.append((f ^ d, lax.ppermute(part, "freq", pairs)))
    return pieces


def make_per_device(n_tile, n_freq):
    def per_device(sources, v_factors, u_factors, tile_ranks, window_bounds):
        v_local = v_factors[0, 0]
        u_local = u_factors[0]
        x_local = sources[0]
        rank_local = tile_ranks[0, :, 0]
        rows = v_local.shape[0]
        use_relay = n_tile == 4 and rows == 2 and u_local.shape[0] == 4
        use_swaps = n_freq & (n_freq - 1) == 0
        count_s = x_local.shape[2]
        chunks = S_CHUNKS if count_s % S_CHUNKS == 0 else 1
        width = count_s // chunks
        received_parts = []
        for c in range(chunks):
            x_part = x_local[:, :, c * width:(c + 1) * width]
            if use_relay:
                spectrum = relay_exchange(v_local, x_part, rank_local, u_local)
            else:
                own = column_products(v_local, x_part, rank_local)
                spectrum = gather_exchange(own, u_local, n_tile)
            if use_swaps:
                received_parts.append(freq_exchange(spectrum, n_freq))
            else:
                received = lax.all_to_all(
                    spectrum[None], "freq", split_axis=2, concat_axis=0, tiled=True
                )
                received_parts.append([(f, received[f]) for f in range(n_freq)])
        pieces = [
            (
                index,
                jnp.concatenate([part[k][1] for part in received_parts], axis=2)
                if chunks > 1
                else piece,
            )
            for k, (index, piece) in enumerate(received_parts[0])
        ]
        cosine_table, sine_table = inverse_tables(n_freq, NT)
        scale = 1.0 / math.sqrt(n_freq)
        count_s = window_bounds.shape[2]
        rows = []
        for index, _ in pieces:
            for table in (cosine_table, sine_table):
                row = lax.dynamic_index_in_dim(table, index, 0, keepdims=False) * scale
                rows.append(jnp.broadcast_to(row[:, None], (NT, count_s)))
        rows = lax.optimization_barrier(rows)
        traces = 0.0
        for k, (_, piece) in enumerate(pieces):
            widened = piece.astype(jnp.float32)
            traces = (
                traces
                + widened[0][:, None, :] * rows[2 * k][None]
                - widened[1][:, None, :] * rows[2 * k + 1][None]
            )
        time_index = jnp.arange(NT, dtype=jnp.int32)[None, :, None]
        inside = (time_index >= window_bounds[0][:, None, :]) & (
            time_index < window_bounds[1][:, None, :]
        )
        return jnp.where(inside, traces, jnp.float32(0.0))

    return per_device


def solution(mesh):
    return jax.shard_map(
        make_per_device(mesh.shape["tile"], mesh.shape["freq"]),
        mesh=mesh,
        in_specs=(
            P("freq", "grp", "tile", None),
            P("freq", "tile", None, "grp", None, None),
            P("freq", None, "grp", None, "tile"),
            P("freq", "grp", "tile"),
            P("grp", ("tile", "freq"), None),
        ),
        out_specs=P(("tile", "freq"), "grp", None),
        check_vma=False,
    )
```

```python
import math

import jax
import jax.numpy as jnp
from jax import lax
from jax.sharding import PartitionSpec as P

NT = 32
S_CHUNKS = 1


first_bin = 2


def inverse_tables(count_freq, count_time):
    freq_index = jnp.arange(count_freq, dtype=jnp.int32)[:, None] + first_bin
    time_index = jnp.arange(count_time, dtype=jnp.int32)[None, :]
    phase_step = freq_index * time_index % count_time
    angles = phase_step.astype(jnp.float32) * (2.0 * math.pi / count_time)
    return (jnp.cos(angles), jnp.sin(angles))


def column_products(v_local, x_local, rank_local):
    products = lax.dot_general(
        v_local, x_local, (((3,), (1,)), ((), ())), preferred_element_type=jnp.float32
    )
    coef_real = products[:, 0, :, 0] - products[:, 1, :, 1]
    coef_imag = products[:, 0, :, 1] + products[:, 1, :, 0]
    slot_index = jnp.arange(v_local.shape[2], dtype=jnp.int32)
    live_slots = slot_index[None, :, None] < rank_local[:, None, None]
    coef_real = jnp.where(live_slots, coef_real, jnp.float32(0.0)).astype(jnp.bfloat16)
    coef_imag = jnp.where(live_slots, coef_imag, jnp.float32(0.0)).astype(jnp.bfloat16)
    return jnp.stack([coef_real, coef_imag], axis=1)


def row_spectrum(u_local, blocks):
    products = lax.dot_general(
        u_local, blocks, (((0, 2), (0, 2)), ((), ())), preferred_element_type=jnp.float32
    )
    real_part = products[0, :, 0] - products[1, :, 1]
    imag_part = products[0, :, 1] + products[1, :, 0]
    return jnp.stack([real_part, imag_part], axis=0).astype(jnp.bfloat16)


def relay_exchange(own, u_local):
    t = lax.axis_index("tile")
    row = t // 2
    mine = lax.dynamic_index_in_dim(own, row, 0, keepdims=False)
    other = lax.dynamic_index_in_dim(own, 1 - row, 0, keepdims=False)
    pairs = [(0, 1), (1, 0), (2, 3), (3, 2)]
    across = lax.ppermute(other, "tile", [(0, 2), (2, 0), (1, 3), (3, 1)])
    partner = lax.ppermute(mine, "tile", pairs)
    passed = lax.ppermute(across, "tile", pairs)
    columns = (t, t ^ 2, t ^ 1, t ^ 3)
    u_order = jnp.stack(
        [lax.dynamic_index_in_dim(u_local, j, 0, keepdims=False) for j in columns], axis=0
    )
    blocks = jnp.stack([mine, across, partner, passed], axis=0)
    return row_spectrum(u_order, blocks)


def gather_exchange(own, u_local, n_tile):
    repeat = n_tile // own.shape[0]
    sending = jnp.repeat(own, repeat, axis=0)
    received = lax.all_to_all(sending, "tile", split_axis=0, concat_axis=0, tiled=True)
    return row_spectrum(u_local, received)


def freq_exchange(spectrum, n_freq):
    f = lax.axis_index("freq")
    width = spectrum.shape[1] // n_freq
    pieces = [(f, lax.dynamic_slice_in_dim(spectrum, f * width, width, axis=1))]
    for d in range(1, n_freq):
        part = lax.dynamic_slice_in_dim(spectrum, (f ^ d) * width, width, axis=1)
        pairs = [(i, i ^ d) for i in range(n_freq)]
        pieces.append((f ^ d, lax.ppermute(part, "freq", pairs)))
    return pieces


def windowed_traces(pieces, window_bounds, n_freq):
    cosine_table, sine_table = inverse_tables(n_freq, NT)
    scale = 1.0 / math.sqrt(n_freq)
    half = NT // 2
    count_m, count_s = window_bounds.shape[1], window_bounds.shape[2]
    rows = []
    for index, _ in pieces:
        for table in (cosine_table, sine_table):
            row = lax.dynamic_index_in_dim(table, index, 0, keepdims=False)[:half] * scale
            rows.append(jnp.broadcast_to(row[:, None], (half, count_s)))
    rows = lax.optimization_barrier(rows)
    sums = [0.0, 0.0]
    for k, (_, piece) in enumerate(pieces):
        widened = piece.astype(jnp.float32)
        sums[k % 2] = (
            sums[k % 2]
            + widened[0][:, None, :] * rows[2 * k][None]
            - widened[1][:, None, :] * rows[2 * k + 1][None]
        )
    even, odd = sums
    if len(pieces) < 2:
        odd = jnp.zeros_like(even)
    even, odd = lax.optimization_barrier((even, odd))
    parity = (pieces[0][0] + first_bin) % 2
    sign = jnp.asarray(1 - 2 * parity, jnp.float32)
    even_weight = jnp.stack([jnp.float32(1.0), sign])[None, :, None, None]
    odd_weight = jnp.stack([jnp.float32(1.0), -sign])[None, :, None, None]
    traces = even[:, None] * even_weight + odd[:, None] * odd_weight
    time_index = (
        jnp.arange(2, dtype=jnp.int32)[:, None] * half + jnp.arange(half, dtype=jnp.int32)[None, :]
    )[None, :, :, None]
    first = window_bounds[0][:, None, None, :]
    last = window_bounds[1][:, None, None, :]
    inside = (time_index >= first) & (time_index < last)
    windowed = jnp.where(inside, traces, jnp.float32(0.0))
    return windowed.reshape(count_m, NT, count_s)


def make_per_device(n_tile, n_freq):
    def per_device(sources, v_factors, u_factors, tile_ranks, window_bounds):
        v_local = v_factors[0, 0]
        u_local = u_factors[0]
        x_local = sources[0]
        rank_local = tile_ranks[0, :, 0]
        rows = v_local.shape[0]
        use_relay = n_tile == 4 and rows == 2 and u_local.shape[0] == 4
        use_swaps = n_freq & (n_freq - 1) == 0
        count_s = x_local.shape[2]
        chunks = S_CHUNKS if count_s % S_CHUNKS == 0 else 1
        width = count_s // chunks
        received_parts = []
        for c in range(chunks):
            x_part = x_local[:, :, c * width:(c + 1) * width]
            own = column_products(v_local, x_part, rank_local)
            if use_relay:
                spectrum = relay_exchange(own, u_local)
            else:
                spectrum = gather_exchange(own, u_local, n_tile)
            if use_swaps:
                received_parts.append(freq_exchange(spectrum, n_freq))
            else:
                received = lax.all_to_all(
                    spectrum[None], "freq", split_axis=2, concat_axis=0, tiled=True
                )
                received_parts.append([(f, received[f]) for f in range(n_freq)])
        pieces = [
            (
                index,
                jnp.concatenate([part[k][1] for part in received_parts], axis=2)
                if chunks > 1
                else piece,
            )
            for k, (index, piece) in enumerate(received_parts[0])
        ]
        return windowed_traces(pieces, window_bounds, n_freq)

    return per_device


def solution(mesh):
    return jax.shard_map(
        make_per_device(mesh.shape["tile"], mesh.shape["freq"]),
        mesh=mesh,
        in_specs=(
            P("freq", "grp", "tile", None),
            P("freq", "tile", None, "grp", None, None),
            P("freq", None, "grp", None, "tile"),
            P("freq", "grp", "tile"),
            P("grp", ("tile", "freq"), None),
        ),
        out_specs=P(("tile", "freq"), "grp", None),
        check_vma=False,
    )
```

```python
import math

import jax
import jax.numpy as jnp
from jax import lax
from jax.sharding import PartitionSpec as P

NT = 32
S_CHUNKS = 1


first_bin = 2


def inverse_tables(count_freq, count_time):
    freq_index = jnp.arange(count_freq, dtype=jnp.int32)[:, None] + first_bin
    time_index = jnp.arange(count_time, dtype=jnp.int32)[None, :]
    phase_step = freq_index * time_index % count_time
    angles = phase_step.astype(jnp.float32) * (2.0 * math.pi / count_time)
    return (jnp.cos(angles), jnp.sin(angles))


def column_products(v_local, x_local, rank_local):
    products = lax.dot_general(
        v_local, x_local, (((3,), (1,)), ((), ())), preferred_element_type=jnp.float32
    )
    coef_real = products[:, 0, :, 0] - products[:, 1, :, 1]
    coef_imag = products[:, 0, :, 1] + products[:, 1, :, 0]
    slot_index = jnp.arange(v_local.shape[2], dtype=jnp.int32)
    live_slots = slot_index[None, :, None] < rank_local[:, None, None]
    coef_real = jnp.where(live_slots, coef_real, jnp.float32(0.0)).astype(jnp.bfloat16)
    coef_imag = jnp.where(live_slots, coef_imag, jnp.float32(0.0)).astype(jnp.bfloat16)
    return jnp.stack([coef_real, coef_imag], axis=1)


def row_spectrum(u_local, blocks):
    products = lax.dot_general(
        u_local, blocks, (((0, 2), (0, 2)), ((), ())), preferred_element_type=jnp.float32
    )
    real_part = products[0, :, 0] - products[1, :, 1]
    imag_part = products[0, :, 1] + products[1, :, 0]
    return jnp.stack([real_part, imag_part], axis=0).astype(jnp.bfloat16)


def row_products(u_part, blocks):
    return lax.dot_general(
        u_part, blocks, (((0, 2), (0, 2)), ((), ())), preferred_element_type=jnp.float32
    )


def finish_spectrum(products):
    real_part = products[0, :, 0] - products[1, :, 1]
    imag_part = products[0, :, 1] + products[1, :, 0]
    return jnp.stack([real_part, imag_part], axis=0).astype(jnp.bfloat16)


def relay_exchange(own, u_local):
    t = lax.axis_index("tile")
    row = t // 2
    mine = lax.dynamic_index_in_dim(own, row, 0, keepdims=False)
    other = lax.dynamic_index_in_dim(own, 1 - row, 0, keepdims=False)
    pairs = [(0, 1), (1, 0), (2, 3), (3, 2)]
    across = lax.ppermute(other, "tile", [(0, 2), (2, 0), (1, 3), (3, 1)])
    partner = lax.ppermute(mine, "tile", pairs)
    passed = lax.ppermute(across, "tile", pairs)
    columns = (t, t ^ 2, t ^ 1, t ^ 3)
    u_order = [lax.dynamic_index_in_dim(u_local, j, 0, keepdims=False) for j in columns]
    early = row_products(
        jnp.stack(u_order[:3], axis=0), jnp.stack([mine, across, partner], axis=0)
    )
    late = row_products(u_order[3][None], passed[None])
    return finish_spectrum(early + late)


def gather_exchange(own, u_local, n_tile):
    repeat = n_tile // own.shape[0]
    sending = jnp.repeat(own, repeat, axis=0)
    received = lax.all_to_all(sending, "tile", split_axis=0, concat_axis=0, tiled=True)
    return row_spectrum(u_local, received)


def freq_exchange(spectrum, n_freq):
    f = lax.axis_index("freq")
    width = spectrum.shape[1] // n_freq
    pieces = [(f, lax.dynamic_slice_in_dim(spectrum, f * width, width, axis=1))]
    for d in range(1, n_freq):
        part = lax.dynamic_slice_in_dim(spectrum, (f ^ d) * width, width, axis=1)
        pairs = [(i, i ^ d) for i in range(n_freq)]
        pieces.append((f ^ d, lax.ppermute(part, "freq", pairs)))
    return pieces


def make_per_device(n_tile, n_freq):
    def per_device(sources, v_factors, u_factors, tile_ranks, window_bounds):
        v_local = v_factors[0, 0]
        u_local = u_factors[0]
        x_local = sources[0]
        rank_local = tile_ranks[0, :, 0]
        rows = v_local.shape[0]
        use_relay = n_tile == 4 and rows == 2 and u_local.shape[0] == 4
        use_swaps = n_freq & (n_freq - 1) == 0
        count_s = x_local.shape[2]
        chunks = S_CHUNKS if count_s % S_CHUNKS == 0 else 1
        width = count_s // chunks
        received_parts = []
        for c in range(chunks):
            x_part = x_local[:, :, c * width:(c + 1) * width]
            own = column_products(v_local, x_part, rank_local)
            if use_relay:
                spectrum = relay_exchange(own, u_local)
            else:
                spectrum = gather_exchange(own, u_local, n_tile)
            if use_swaps:
                received_parts.append(freq_exchange(spectrum, n_freq))
            else:
                received = lax.all_to_all(
                    spectrum[None], "freq", split_axis=2, concat_axis=0, tiled=True
                )
                received_parts.append([(f, received[f]) for f in range(n_freq)])
        pieces = [
            (
                index,
                jnp.concatenate([part[k][1] for part in received_parts], axis=2)
                if chunks > 1
                else piece,
            )
            for k, (index, piece) in enumerate(received_parts[0])
        ]
        cosine_table, sine_table = inverse_tables(n_freq, NT)
        scale = 1.0 / math.sqrt(n_freq)
        count_s = window_bounds.shape[2]
        rows = []
        for index, _ in pieces:
            for table in (cosine_table, sine_table):
                row = lax.dynamic_index_in_dim(table, index, 0, keepdims=False) * scale
                rows.append(jnp.broadcast_to(row[:, None], (NT, count_s)))
        rows = lax.optimization_barrier(rows)
        traces = 0.0
        for k, (_, piece) in enumerate(pieces):
            widened = piece.astype(jnp.float32)
            traces = (
                traces
                + widened[0][:, None, :] * rows[2 * k][None]
                - widened[1][:, None, :] * rows[2 * k + 1][None]
            )
        time_index = jnp.arange(NT, dtype=jnp.int32)[None, :, None]
        inside = (time_index >= window_bounds[0][:, None, :]) & (
            time_index < window_bounds[1][:, None, :]
        )
        return jnp.where(inside, traces, jnp.float32(0.0))

    return per_device


def solution(mesh):
    return jax.shard_map(
        make_per_device(mesh.shape["tile"], mesh.shape["freq"]),
        mesh=mesh,
        in_specs=(
            P("freq", "grp", "tile", None),
            P("freq", "tile", None, "grp", None, None),
            P("freq", None, "grp", None, "tile"),
            P("freq", "grp", "tile"),
            P("grp", ("tile", "freq"), None),
        ),
        out_specs=P(("tile", "freq"), "grp", None),
        check_vma=False,
    )
```

```python
import math

import jax
import jax.numpy as jnp
from jax import lax
from jax.sharding import PartitionSpec as P

NT = 32
S_CHUNKS = 1


first_bin = 2


def inverse_tables(count_freq, count_time):
    freq_index = jnp.arange(count_freq, dtype=jnp.int32)[:, None] + first_bin
    time_index = jnp.arange(count_time, dtype=jnp.int32)[None, :]
    phase_step = freq_index * time_index % count_time
    angles = phase_step.astype(jnp.float32) * (2.0 * math.pi / count_time)
    return (jnp.cos(angles), jnp.sin(angles))


def column_products(v_local, x_local, rank_local):
    v_real, v_imag = v_local[:, 0], v_local[:, 1]
    stacked = jnp.stack(
        [
            jnp.concatenate([v_real, -v_imag], axis=-1),
            jnp.concatenate([v_imag, v_real], axis=-1),
        ],
        axis=1,
    )
    x_both = x_local.reshape(x_local.shape[0] * x_local.shape[1], x_local.shape[2])
    products = lax.dot_general(
        stacked, x_both, (((3,), (0,)), ((), ())), preferred_element_type=jnp.float32
    )
    slot_index = jnp.arange(v_local.shape[2], dtype=jnp.int32)
    live_slots = slot_index[None, None, :, None] < rank_local[:, None, None, None]
    return jnp.where(live_slots, products, jnp.float32(0.0)).astype(jnp.bfloat16)


def row_spectrum(u_local, blocks):
    products = lax.dot_general(
        u_local, blocks, (((0, 2), (0, 2)), ((), ())), preferred_element_type=jnp.float32
    )
    real_part = products[0, :, 0] - products[1, :, 1]
    imag_part = products[0, :, 1] + products[1, :, 0]
    return jnp.stack([real_part, imag_part], axis=0).astype(jnp.bfloat16)


def row_products(u_part, blocks):
    return lax.dot_general(
        u_part, blocks, (((0, 2), (0, 2)), ((), ())), preferred_element_type=jnp.float32
    )


def finish_spectrum(products):
    real_part = products[0, :, 0] - products[1, :, 1]
    imag_part = products[0, :, 1] + products[1, :, 0]
    return jnp.stack([real_part, imag_part], axis=0).astype(jnp.bfloat16)


def relay_exchange(own, u_local):
    t = lax.axis_index("tile")
    row = t // 2
    mine = lax.dynamic_index_in_dim(own, row, 0, keepdims=False)
    other = lax.dynamic_index_in_dim(own, 1 - row, 0, keepdims=False)
    pairs = [(0, 1), (1, 0), (2, 3), (3, 2)]
    across = lax.ppermute(other, "tile", [(0, 2), (2, 0), (1, 3), (3, 1)])
    partner = lax.ppermute(mine, "tile", pairs)
    passed = lax.ppermute(across, "tile", pairs)
    columns = (t, t ^ 2, t ^ 1, t ^ 3)
    u_order = [lax.dynamic_index_in_dim(u_local, j, 0, keepdims=False) for j in columns]
    early = row_products(
        jnp.stack(u_order[:3], axis=0), jnp.stack([mine, across, partner], axis=0)
    )
    late = row_products(u_order[3][None], passed[None])
    return finish_spectrum(early + late)


def gather_exchange(own, u_local, n_tile):
    repeat = n_tile // own.shape[0]
    sending = jnp.repeat(own, repeat, axis=0)
    received = lax.all_to_all(sending, "tile", split_axis=0, concat_axis=0, tiled=True)
    return row_spectrum(u_local, received)


def freq_exchange(spectrum, n_freq):
    f = lax.axis_index("freq")
    width = spectrum.shape[1] // n_freq
    pieces = [(f, lax.dynamic_slice_in_dim(spectrum, f * width, width, axis=1))]
    for d in range(1, n_freq):
        part = lax.dynamic_slice_in_dim(spectrum, (f ^ d) * width, width, axis=1)
        pairs = [(i, i ^ d) for i in range(n_freq)]
        pieces.append((f ^ d, lax.ppermute(part, "freq", pairs)))
    return pieces


def make_per_device(n_tile, n_freq):
    def per_device(sources, v_factors, u_factors, tile_ranks, window_bounds):
        v_local = v_factors[0, 0]
        u_local = u_factors[0]
        x_local = sources[0]
        rank_local = tile_ranks[0, :, 0]
        rows = v_local.shape[0]
        use_relay = n_tile == 4 and rows == 2 and u_local.shape[0] == 4
        use_swaps = n_freq & (n_freq - 1) == 0
        count_s = x_local.shape[2]
        chunks = S_CHUNKS if count_s % S_CHUNKS == 0 else 1
        width = count_s // chunks
        received_parts = []
        for c in range(chunks):
            x_part = x_local[:, :, c * width:(c + 1) * width]
            own = column_products(v_local, x_part, rank_local)
            if use_relay:
                spectrum = relay_exchange(own, u_local)
            else:
                spectrum = gather_exchange(own, u_local, n_tile)
            if use_swaps:
                received_parts.append(freq_exchange(spectrum, n_freq))
            else:
                received = lax.all_to_all(
                    spectrum[None], "freq", split_axis=2, concat_axis=0, tiled=True
                )
                received_parts.append([(f, received[f]) for f in range(n_freq)])
        pieces = [
            (
                index,
                jnp.concatenate([part[k][1] for part in received_parts], axis=2)
                if chunks > 1
                else piece,
            )
            for k, (index, piece) in enumerate(received_parts[0])
        ]
        cosine_table, sine_table = inverse_tables(n_freq, NT)
        scale = 1.0 / math.sqrt(n_freq)
        count_s = window_bounds.shape[2]
        rows = []
        for index, _ in pieces:
            for table in (cosine_table, sine_table):
                row = lax.dynamic_index_in_dim(table, index, 0, keepdims=False) * scale
                rows.append(jnp.broadcast_to(row[:, None], (NT, count_s)))
        rows = lax.optimization_barrier(rows)
        traces = 0.0
        for k, (_, piece) in enumerate(pieces):
            widened = piece.astype(jnp.float32)
            traces = (
                traces
                + widened[0][:, None, :] * rows[2 * k][None]
                - widened[1][:, None, :] * rows[2 * k + 1][None]
            )
        time_index = jnp.arange(NT, dtype=jnp.int32)[None, :, None]
        inside = (time_index >= window_bounds[0][:, None, :]) & (
            time_index < window_bounds[1][:, None, :]
        )
        return jnp.where(inside, traces, jnp.float32(0.0))

    return per_device


def solution(mesh):
    return jax.shard_map(
        make_per_device(mesh.shape["tile"], mesh.shape["freq"]),
        mesh=mesh,
        in_specs=(
            P("freq", "grp", "tile", None),
            P("freq", "tile", None, "grp", None, None),
            P("freq", None, "grp", None, "tile"),
            P("freq", "grp", "tile"),
            P("grp", ("tile", "freq"), None),
        ),
        out_specs=P(("tile", "freq"), "grp", None),
        check_vma=False,
    )
```

```python
import math

import jax
import jax.numpy as jnp
from jax import lax
from jax.sharding import PartitionSpec as P

NT = 32
S_CHUNKS = 1


first_bin = 2


def inverse_tables(count_freq, count_time):
    freq_index = jnp.arange(count_freq, dtype=jnp.int32)[:, None] + first_bin
    time_index = jnp.arange(count_time, dtype=jnp.int32)[None, :]
    phase_step = freq_index * time_index % count_time
    angles = phase_step.astype(jnp.float32) * (2.0 * math.pi / count_time)
    return (jnp.cos(angles), jnp.sin(angles))


def column_products(v_local, x_local, rank_local):
    x_real, x_imag = x_local[0], x_local[1]
    x_both = jnp.stack(
        [jnp.stack([x_real, x_imag], axis=1), jnp.stack([-x_imag, x_real], axis=1)], axis=0
    )
    products = lax.dot_general(
        v_local, x_both, (((1, 3), (0, 1)), ((), ())), preferred_element_type=jnp.float32
    )
    products = products.transpose(0, 2, 1, 3)
    slot_index = jnp.arange(v_local.shape[2], dtype=jnp.int32)
    live_slots = slot_index[None, None, :, None] < rank_local[:, None, None, None]
    return jnp.where(live_slots, products, jnp.float32(0.0)).astype(jnp.bfloat16)


def row_spectrum(u_local, blocks):
    products = lax.dot_general(
        u_local, blocks, (((0, 2), (0, 2)), ((), ())), preferred_element_type=jnp.float32
    )
    real_part = products[0, :, 0] - products[1, :, 1]
    imag_part = products[0, :, 1] + products[1, :, 0]
    return jnp.stack([real_part, imag_part], axis=0).astype(jnp.bfloat16)


def row_products(u_part, blocks):
    return lax.dot_general(
        u_part, blocks, (((0, 2), (0, 2)), ((), ())), preferred_element_type=jnp.float32
    )


def finish_spectrum(products):
    real_part = products[0, :, 0] - products[1, :, 1]
    imag_part = products[0, :, 1] + products[1, :, 0]
    return jnp.stack([real_part, imag_part], axis=0).astype(jnp.bfloat16)


def relay_exchange(own, u_local):
    t = lax.axis_index("tile")
    row = t // 2
    mine = lax.dynamic_index_in_dim(own, row, 0, keepdims=False)
    other = lax.dynamic_index_in_dim(own, 1 - row, 0, keepdims=False)
    pairs = [(0, 1), (1, 0), (2, 3), (3, 2)]
    across = lax.ppermute(other, "tile", [(0, 2), (2, 0), (1, 3), (3, 1)])
    partner = lax.ppermute(mine, "tile", pairs)
    passed = lax.ppermute(across, "tile", pairs)
    columns = (t, t ^ 2, t ^ 1, t ^ 3)
    u_order = [lax.dynamic_index_in_dim(u_local, j, 0, keepdims=False) for j in columns]
    early = row_products(
        jnp.stack(u_order[:3], axis=0), jnp.stack([mine, across, partner], axis=0)
    )
    late = row_products(u_order[3][None], passed[None])
    return finish_spectrum(early + late)


def gather_exchange(own, u_local, n_tile):
    repeat = n_tile // own.shape[0]
    sending = jnp.repeat(own, repeat, axis=0)
    received = lax.all_to_all(sending, "tile", split_axis=0, concat_axis=0, tiled=True)
    return row_spectrum(u_local, received)


def freq_exchange(spectrum, n_freq):
    f = lax.axis_index("freq")
    width = spectrum.shape[1] // n_freq
    pieces = [(f, lax.dynamic_slice_in_dim(spectrum, f * width, width, axis=1))]
    for d in range(1, n_freq):
        part = lax.dynamic_slice_in_dim(spectrum, (f ^ d) * width, width, axis=1)
        pairs = [(i, i ^ d) for i in range(n_freq)]
        pieces.append((f ^ d, lax.ppermute(part, "freq", pairs)))
    return pieces


def make_per_device(n_tile, n_freq):
    def per_device(sources, v_factors, u_factors, tile_ranks, window_bounds):
        v_local = v_factors[0, 0]
        u_local = u_factors[0]
        x_local = sources[0]
        rank_local = tile_ranks[0, :, 0]
        rows = v_local.shape[0]
        use_relay = n_tile == 4 and rows == 2 and u_local.shape[0] == 4
        use_swaps = n_freq & (n_freq - 1) == 0
        count_s = x_local.shape[2]
        chunks = S_CHUNKS if count_s % S_CHUNKS == 0 else 1
        width = count_s // chunks
        received_parts = []
        for c in range(chunks):
            x_part = x_local[:, :, c * width:(c + 1) * width]
            own = column_products(v_local, x_part, rank_local)
            if use_relay:
                spectrum = relay_exchange(own, u_local)
            else:
                spectrum = gather_exchange(own, u_local, n_tile)
            if use_swaps:
                received_parts.append(freq_exchange(spectrum, n_freq))
            else:
                received = lax.all_to_all(
                    spectrum[None], "freq", split_axis=2, concat_axis=0, tiled=True
                )
                received_parts.append([(f, received[f]) for f in range(n_freq)])
        pieces = [
            (
                index,
                jnp.concatenate([part[k][1] for part in received_parts], axis=2)
                if chunks > 1
                else piece,
            )
            for k, (index, piece) in enumerate(received_parts[0])
        ]
        cosine_table, sine_table = inverse_tables(n_freq, NT)
        scale = 1.0 / math.sqrt(n_freq)
        count_s = window_bounds.shape[2]
        rows = []
        for index, _ in pieces:
            for table in (cosine_table, sine_table):
                row = lax.dynamic_index_in_dim(table, index, 0, keepdims=False) * scale
                rows.append(jnp.broadcast_to(row[:, None], (NT, count_s)))
        rows = lax.optimization_barrier(rows)
        traces = 0.0
        for k, (_, piece) in enumerate(pieces):
            widened = piece.astype(jnp.float32)
            traces = (
                traces
                + widened[0][:, None, :] * rows[2 * k][None]
                - widened[1][:, None, :] * rows[2 * k + 1][None]
            )
        time_index = jnp.arange(NT, dtype=jnp.int32)[None, :, None]
        inside = (time_index >= window_bounds[0][:, None, :]) & (
            time_index < window_bounds[1][:, None, :]
        )
        return jnp.where(inside, traces, jnp.float32(0.0))

    return per_device


def solution(mesh):
    return jax.shard_map(
        make_per_device(mesh.shape["tile"], mesh.shape["freq"]),
        mesh=mesh,
        in_specs=(
            P("freq", "grp", "tile", None),
            P("freq", "tile", None, "grp", None, None),
            P("freq", None, "grp", None, "tile"),
            P("freq", "grp", "tile"),
            P("grp", ("tile", "freq"), None),
        ),
        out_specs=P(("tile", "freq"), "grp", None),
        check_vma=False,
    )
```

```python
import math

import jax
import jax.numpy as jnp
from jax import lax
from jax.sharding import PartitionSpec as P

NT = 32
S_CHUNKS = 1


first_bin = 2


def inverse_tables(count_freq, count_time):
    freq_index = jnp.arange(count_freq, dtype=jnp.int32)[:, None] + first_bin
    time_index = jnp.arange(count_time, dtype=jnp.int32)[None, :]
    phase_step = freq_index * time_index % count_time
    angles = phase_step.astype(jnp.float32) * (2.0 * math.pi / count_time)
    return (jnp.cos(angles), jnp.sin(angles))


def column_products(v_local, x_local, rank_local):
    v_real, v_imag = v_local[:, 0], v_local[:, 1]
    stacked = jnp.stack(
        [
            jnp.concatenate([v_real, -v_imag], axis=-1),
            jnp.concatenate([v_imag, v_real], axis=-1),
        ],
        axis=1,
    )
    stacked = lax.optimization_barrier(stacked)
    x_both = x_local.reshape(x_local.shape[0] * x_local.shape[1], x_local.shape[2])
    products = lax.dot_general(
        stacked, x_both, (((3,), (0,)), ((), ())), preferred_element_type=jnp.float32
    )
    slot_index = jnp.arange(v_local.shape[2], dtype=jnp.int32)
    live_slots = slot_index[None, None, :, None] < rank_local[:, None, None, None]
    return jnp.where(live_slots, products, jnp.float32(0.0)).astype(jnp.bfloat16)


def row_spectrum(u_local, blocks):
    products = lax.dot_general(
        u_local, blocks, (((0, 2), (0, 2)), ((), ())), preferred_element_type=jnp.float32
    )
    real_part = products[0, :, 0] - products[1, :, 1]
    imag_part = products[0, :, 1] + products[1, :, 0]
    return jnp.stack([real_part, imag_part], axis=0).astype(jnp.bfloat16)


def row_products(u_part, blocks):
    return lax.dot_general(
        u_part, blocks, (((0, 2), (0, 2)), ((), ())), preferred_element_type=jnp.float32
    )


def finish_spectrum(products):
    real_part = products[0, :, 0] - products[1, :, 1]
    imag_part = products[0, :, 1] + products[1, :, 0]
    return jnp.stack([real_part, imag_part], axis=0).astype(jnp.bfloat16)


def relay_exchange(own, u_local):
    t = lax.axis_index("tile")
    row = t // 2
    mine = lax.dynamic_index_in_dim(own, row, 0, keepdims=False)
    other = lax.dynamic_index_in_dim(own, 1 - row, 0, keepdims=False)
    pairs = [(0, 1), (1, 0), (2, 3), (3, 2)]
    across = lax.ppermute(other, "tile", [(0, 2), (2, 0), (1, 3), (3, 1)])
    partner = lax.ppermute(mine, "tile", pairs)
    passed = lax.ppermute(across, "tile", pairs)
    columns = (t, t ^ 2, t ^ 1, t ^ 3)
    u_order = [lax.dynamic_index_in_dim(u_local, j, 0, keepdims=False) for j in columns]
    early = row_products(
        jnp.stack(u_order[:3], axis=0), jnp.stack([mine, across, partner], axis=0)
    )
    late = row_products(u_order[3][None], passed[None])
    return finish_spectrum(early + late)


def gather_exchange(own, u_local, n_tile):
    repeat = n_tile // own.shape[0]
    sending = jnp.repeat(own, repeat, axis=0)
    received = lax.all_to_all(sending, "tile", split_axis=0, concat_axis=0, tiled=True)
    return row_spectrum(u_local, received)


def freq_exchange(spectrum, n_freq):
    f = lax.axis_index("freq")
    width = spectrum.shape[1] // n_freq
    pieces = [(f, lax.dynamic_slice_in_dim(spectrum, f * width, width, axis=1))]
    for d in range(1, n_freq):
        part = lax.dynamic_slice_in_dim(spectrum, (f ^ d) * width, width, axis=1)
        pairs = [(i, i ^ d) for i in range(n_freq)]
        pieces.append((f ^ d, lax.ppermute(part, "freq", pairs)))
    return pieces


def make_per_device(n_tile, n_freq):
    def per_device(sources, v_factors, u_factors, tile_ranks, window_bounds):
        v_local = v_factors[0, 0]
        u_local = u_factors[0]
        x_local = sources[0]
        rank_local = tile_ranks[0, :, 0]
        rows = v_local.shape[0]
        use_relay = n_tile == 4 and rows == 2 and u_local.shape[0] == 4
        use_swaps = n_freq & (n_freq - 1) == 0
        count_s = x_local.shape[2]
        chunks = S_CHUNKS if count_s % S_CHUNKS == 0 else 1
        width = count_s // chunks
        received_parts = []
        for c in range(chunks):
            x_part = x_local[:, :, c * width:(c + 1) * width]
            own = column_products(v_local, x_part, rank_local)
            if use_relay:
                spectrum = relay_exchange(own, u_local)
            else:
                spectrum = gather_exchange(own, u_local, n_tile)
            if use_swaps:
                received_parts.append(freq_exchange(spectrum, n_freq))
            else:
                received = lax.all_to_all(
                    spectrum[None], "freq", split_axis=2, concat_axis=0, tiled=True
                )
                received_parts.append([(f, received[f]) for f in range(n_freq)])
        pieces = [
            (
                index,
                jnp.concatenate([part[k][1] for part in received_parts], axis=2)
                if chunks > 1
                else piece,
            )
            for k, (index, piece) in enumerate(received_parts[0])
        ]
        cosine_table, sine_table = inverse_tables(n_freq, NT)
        scale = 1.0 / math.sqrt(n_freq)
        count_s = window_bounds.shape[2]
        rows = []
        for index, _ in pieces:
            for table in (cosine_table, sine_table):
                row = lax.dynamic_index_in_dim(table, index, 0, keepdims=False) * scale
                rows.append(jnp.broadcast_to(row[:, None], (NT, count_s)))
        rows = lax.optimization_barrier(rows)
        traces = 0.0
        for k, (_, piece) in enumerate(pieces):
            widened = piece.astype(jnp.float32)
            traces = (
                traces
                + widened[0][:, None, :] * rows[2 * k][None]
                - widened[1][:, None, :] * rows[2 * k + 1][None]
            )
        time_index = jnp.arange(NT, dtype=jnp.int32)[None, :, None]
        inside = (time_index >= window_bounds[0][:, None, :]) & (
            time_index < window_bounds[1][:, None, :]
        )
        return jnp.where(inside, traces, jnp.float32(0.0))

    return per_device


def solution(mesh):
    return jax.shard_map(
        make_per_device(mesh.shape["tile"], mesh.shape["freq"]),
        mesh=mesh,
        in_specs=(
            P("freq", "grp", "tile", None),
            P("freq", "tile", None, "grp", None, None),
            P("freq", None, "grp", None, "tile"),
            P("freq", "grp", "tile"),
            P("grp", ("tile", "freq"), None),
        ),
        out_specs=P(("tile", "freq"), "grp", None),
        check_vma=False,
    )
```

```python
import math

import jax
import jax.numpy as jnp
from jax import lax
from jax.sharding import PartitionSpec as P

NT = 32
S_CHUNKS = 1


first_bin = 2


def inverse_tables(count_freq, count_time):
    freq_index = jnp.arange(count_freq, dtype=jnp.int32)[:, None] + first_bin
    time_index = jnp.arange(count_time, dtype=jnp.int32)[None, :]
    phase_step = freq_index * time_index % count_time
    angles = phase_step.astype(jnp.float32) * (2.0 * math.pi / count_time)
    return (jnp.cos(angles), jnp.sin(angles))


def column_products(v_local, x_local, rank_local):
    part_sign = jnp.array([1.0, -1.0], jnp.bfloat16)[None, :, None, None]
    stacked = jnp.stack([v_local * part_sign, v_local[:, ::-1]], axis=1)
    products = lax.dot_general(
        stacked, x_local, (((2, 4), (0, 1)), ((), ())), preferred_element_type=jnp.float32
    )
    slot_index = jnp.arange(v_local.shape[2], dtype=jnp.int32)
    live_slots = slot_index[None, None, :, None] < rank_local[:, None, None, None]
    return jnp.where(live_slots, products, jnp.float32(0.0)).astype(jnp.bfloat16)


def row_spectrum(u_local, blocks):
    products = lax.dot_general(
        u_local, blocks, (((0, 2), (0, 2)), ((), ())), preferred_element_type=jnp.float32
    )
    real_part = products[0, :, 0] - products[1, :, 1]
    imag_part = products[0, :, 1] + products[1, :, 0]
    return jnp.stack([real_part, imag_part], axis=0).astype(jnp.bfloat16)


def row_products(u_part, blocks):
    return lax.dot_general(
        u_part, blocks, (((0, 2), (0, 2)), ((), ())), preferred_element_type=jnp.float32
    )


def finish_spectrum(products):
    real_part = products[0, :, 0] - products[1, :, 1]
    imag_part = products[0, :, 1] + products[1, :, 0]
    return jnp.stack([real_part, imag_part], axis=0).astype(jnp.bfloat16)


def relay_exchange(own, u_local):
    t = lax.axis_index("tile")
    row = t // 2
    mine = lax.dynamic_index_in_dim(own, row, 0, keepdims=False)
    other = lax.dynamic_index_in_dim(own, 1 - row, 0, keepdims=False)
    pairs = [(0, 1), (1, 0), (2, 3), (3, 2)]
    across = lax.ppermute(other, "tile", [(0, 2), (2, 0), (1, 3), (3, 1)])
    partner = lax.ppermute(mine, "tile", pairs)
    passed = lax.ppermute(across, "tile", pairs)
    columns = (t, t ^ 2, t ^ 1, t ^ 3)
    u_order = [lax.dynamic_index_in_dim(u_local, j, 0, keepdims=False) for j in columns]
    early = row_products(
        jnp.stack(u_order[:3], axis=0), jnp.stack([mine, across, partner], axis=0)
    )
    late = row_products(u_order[3][None], passed[None])
    return finish_spectrum(early + late)


def gather_exchange(own, u_local, n_tile):
    repeat = n_tile // own.shape[0]
    sending = jnp.repeat(own, repeat, axis=0)
    received = lax.all_to_all(sending, "tile", split_axis=0, concat_axis=0, tiled=True)
    return row_spectrum(u_local, received)


def freq_exchange(spectrum, n_freq):
    f = lax.axis_index("freq")
    width = spectrum.shape[1] // n_freq
    pieces = [(f, lax.dynamic_slice_in_dim(spectrum, f * width, width, axis=1))]
    for d in range(1, n_freq):
        part = lax.dynamic_slice_in_dim(spectrum, (f ^ d) * width, width, axis=1)
        pairs = [(i, i ^ d) for i in range(n_freq)]
        pieces.append((f ^ d, lax.ppermute(part, "freq", pairs)))
    return pieces


def make_per_device(n_tile, n_freq):
    def per_device(sources, v_factors, u_factors, tile_ranks, window_bounds):
        v_local = v_factors[0, 0]
        u_local = u_factors[0]
        x_local = sources[0]
        rank_local = tile_ranks[0, :, 0]
        rows = v_local.shape[0]
        use_relay = n_tile == 4 and rows == 2 and u_local.shape[0] == 4
        use_swaps = n_freq & (n_freq - 1) == 0
        count_s = x_local.shape[2]
        chunks = S_CHUNKS if count_s % S_CHUNKS == 0 else 1
        width = count_s // chunks
        received_parts = []
        for c in range(chunks):
            x_part = x_local[:, :, c * width:(c + 1) * width]
            own = column_products(v_local, x_part, rank_local)
            if use_relay:
                spectrum = relay_exchange(own, u_local)
            else:
                spectrum = gather_exchange(own, u_local, n_tile)
            if use_swaps:
                received_parts.append(freq_exchange(spectrum, n_freq))
            else:
                received = lax.all_to_all(
                    spectrum[None], "freq", split_axis=2, concat_axis=0, tiled=True
                )
                received_parts.append([(f, received[f]) for f in range(n_freq)])
        pieces = [
            (
                index,
                jnp.concatenate([part[k][1] for part in received_parts], axis=2)
                if chunks > 1
                else piece,
            )
            for k, (index, piece) in enumerate(received_parts[0])
        ]
        cosine_table, sine_table = inverse_tables(n_freq, NT)
        scale = 1.0 / math.sqrt(n_freq)
        count_s = window_bounds.shape[2]
        rows = []
        for index, _ in pieces:
            for table in (cosine_table, sine_table):
                row = lax.dynamic_index_in_dim(table, index, 0, keepdims=False) * scale
                rows.append(jnp.broadcast_to(row[:, None], (NT, count_s)))
        rows = lax.optimization_barrier(rows)
        traces = 0.0
        for k, (_, piece) in enumerate(pieces):
            widened = piece.astype(jnp.float32)
            traces = (
                traces
                + widened[0][:, None, :] * rows[2 * k][None]
                - widened[1][:, None, :] * rows[2 * k + 1][None]
            )
        time_index = jnp.arange(NT, dtype=jnp.int32)[None, :, None]
        inside = (time_index >= window_bounds[0][:, None, :]) & (
            time_index < window_bounds[1][:, None, :]
        )
        return jnp.where(inside, traces, jnp.float32(0.0))

    return per_device


def solution(mesh):
    return jax.shard_map(
        make_per_device(mesh.shape["tile"], mesh.shape["freq"]),
        mesh=mesh,
        in_specs=(
            P("freq", "grp", "tile", None),
            P("freq", "tile", None, "grp", None, None),
            P("freq", None, "grp", None, "tile"),
            P("freq", "grp", "tile"),
            P("grp", ("tile", "freq"), None),
        ),
        out_specs=P(("tile", "freq"), "grp", None),
        check_vma=False,
    )
```

```python
import math

import jax
import jax.numpy as jnp
from jax import lax
from jax.sharding import PartitionSpec as P

NT = 32
S_CHUNKS = 1


first_bin = 2


def inverse_tables(count_freq, count_time):
    freq_index = jnp.arange(count_freq, dtype=jnp.int32)[:, None] + first_bin
    time_index = jnp.arange(count_time, dtype=jnp.int32)[None, :]
    phase_step = freq_index * time_index % count_time
    angles = phase_step.astype(jnp.float32) * (2.0 * math.pi / count_time)
    return (jnp.cos(angles), jnp.sin(angles))


def column_products(v_local, x_local, rank_local):
    slot_index = jnp.arange(v_local.shape[2], dtype=jnp.int32)
    live_slots = slot_index[None, None, :, None] < rank_local[:, None, None, None]
    v_live = jnp.where(live_slots, v_local, jnp.zeros((), v_local.dtype))
    v_real, v_imag = v_live[:, 0], v_live[:, 1]
    stacked = jnp.stack(
        [
            jnp.concatenate([v_real, -v_imag], axis=-1),
            jnp.concatenate([v_imag, v_real], axis=-1),
        ],
        axis=1,
    )
    x_both = x_local.reshape(x_local.shape[0] * x_local.shape[1], x_local.shape[2])
    products = lax.dot_general(
        stacked, x_both, (((3,), (0,)), ((), ())), preferred_element_type=jnp.float32
    )
    return products.astype(jnp.bfloat16)


def row_spectrum(u_local, blocks):
    products = lax.dot_general(
        u_local, blocks, (((0, 2), (0, 2)), ((), ())), preferred_element_type=jnp.float32
    )
    real_part = products[0, :, 0] - products[1, :, 1]
    imag_part = products[0, :, 1] + products[1, :, 0]
    return jnp.stack([real_part, imag_part], axis=0).astype(jnp.bfloat16)


def row_products(u_part, blocks):
    return lax.dot_general(
        u_part, blocks, (((0, 2), (0, 2)), ((), ())), preferred_element_type=jnp.float32
    )


def finish_spectrum(products):
    real_part = products[0, :, 0] - products[1, :, 1]
    imag_part = products[0, :, 1] + products[1, :, 0]
    return jnp.stack([real_part, imag_part], axis=0).astype(jnp.bfloat16)


def relay_exchange(own, u_local):
    t = lax.axis_index("tile")
    row = t // 2
    mine = lax.dynamic_index_in_dim(own, row, 0, keepdims=False)
    other = lax.dynamic_index_in_dim(own, 1 - row, 0, keepdims=False)
    pairs = [(0, 1), (1, 0), (2, 3), (3, 2)]
    across = lax.ppermute(other, "tile", [(0, 2), (2, 0), (1, 3), (3, 1)])
    partner = lax.ppermute(mine, "tile", pairs)
    passed = lax.ppermute(across, "tile", pairs)
    columns = (t, t ^ 2, t ^ 1, t ^ 3)
    u_order = [lax.dynamic_index_in_dim(u_local, j, 0, keepdims=False) for j in columns]
    early = row_products(
        jnp.stack(u_order[:3], axis=0), jnp.stack([mine, across, partner], axis=0)
    )
    late = row_products(u_order[3][None], passed[None])
    return finish_spectrum(early + late)


def gather_exchange(own, u_local, n_tile):
    repeat = n_tile // own.shape[0]
    sending = jnp.repeat(own, repeat, axis=0)
    received = lax.all_to_all(sending, "tile", split_axis=0, concat_axis=0, tiled=True)
    return row_spectrum(u_local, received)


def freq_exchange(spectrum, n_freq):
    f = lax.axis_index("freq")
    width = spectrum.shape[1] // n_freq
    pieces = [(f, lax.dynamic_slice_in_dim(spectrum, f * width, width, axis=1))]
    for d in range(1, n_freq):
        part = lax.dynamic_slice_in_dim(spectrum, (f ^ d) * width, width, axis=1)
        pairs = [(i, i ^ d) for i in range(n_freq)]
        pieces.append((f ^ d, lax.ppermute(part, "freq", pairs)))
    return pieces


def make_per_device(n_tile, n_freq):
    def per_device(sources, v_factors, u_factors, tile_ranks, window_bounds):
        v_local = v_factors[0, 0]
        u_local = u_factors[0]
        x_local = sources[0]
        rank_local = tile_ranks[0, :, 0]
        rows = v_local.shape[0]
        use_relay = n_tile == 4 and rows == 2 and u_local.shape[0] == 4
        use_swaps = n_freq & (n_freq - 1) == 0
        count_s = x_local.shape[2]
        chunks = S_CHUNKS if count_s % S_CHUNKS == 0 else 1
        width = count_s // chunks
        received_parts = []
        for c in range(chunks):
            x_part = x_local[:, :, c * width:(c + 1) * width]
            own = column_products(v_local, x_part, rank_local)
            if use_relay:
                spectrum = relay_exchange(own, u_local)
            else:
                spectrum = gather_exchange(own, u_local, n_tile)
            if use_swaps:
                received_parts.append(freq_exchange(spectrum, n_freq))
            else:
                received = lax.all_to_all(
                    spectrum[None], "freq", split_axis=2, concat_axis=0, tiled=True
                )
                received_parts.append([(f, received[f]) for f in range(n_freq)])
        pieces = [
            (
                index,
                jnp.concatenate([part[k][1] for part in received_parts], axis=2)
                if chunks > 1
                else piece,
            )
            for k, (index, piece) in enumerate(received_parts[0])
        ]
        cosine_table, sine_table = inverse_tables(n_freq, NT)
        scale = 1.0 / math.sqrt(n_freq)
        count_s = window_bounds.shape[2]
        rows = []
        for index, _ in pieces:
            for table in (cosine_table, sine_table):
                row = lax.dynamic_index_in_dim(table, index, 0, keepdims=False) * scale
                rows.append(jnp.broadcast_to(row[:, None], (NT, count_s)))
        rows = lax.optimization_barrier(rows)
        traces = 0.0
        for k, (_, piece) in enumerate(pieces):
            widened = piece.astype(jnp.float32)
            traces = (
                traces
                + widened[0][:, None, :] * rows[2 * k][None]
                - widened[1][:, None, :] * rows[2 * k + 1][None]
            )
        time_index = jnp.arange(NT, dtype=jnp.int32)[None, :, None]
        inside = (time_index >= window_bounds[0][:, None, :]) & (
            time_index < window_bounds[1][:, None, :]
        )
        return jnp.where(inside, traces, jnp.float32(0.0))

    return per_device


def solution(mesh):
    return jax.shard_map(
        make_per_device(mesh.shape["tile"], mesh.shape["freq"]),
        mesh=mesh,
        in_specs=(
            P("freq", "grp", "tile", None),
            P("freq", "tile", None, "grp", None, None),
            P("freq", None, "grp", None, "tile"),
            P("freq", "grp", "tile"),
            P("grp", ("tile", "freq"), None),
        ),
        out_specs=P(("tile", "freq"), "grp", None),
        check_vma=False,
    )
```

```python
import math

import jax
import jax.numpy as jnp
from jax import lax
from jax.sharding import PartitionSpec as P

NT = 32
S_CHUNKS = 1


first_bin = 2


def inverse_tables(count_freq, count_time):
    freq_index = jnp.arange(count_freq, dtype=jnp.int32)[:, None] + first_bin
    time_index = jnp.arange(count_time, dtype=jnp.int32)[None, :]
    phase_step = freq_index * time_index % count_time
    angles = phase_step.astype(jnp.float32) * (2.0 * math.pi / count_time)
    return (jnp.cos(angles), jnp.sin(angles))


def column_products(v_local, x_local, rank_local):
    v_real, v_imag = v_local[:, 0], v_local[:, 1]
    stacked = jnp.stack(
        [
            jnp.concatenate([v_real, -v_imag], axis=-1),
            jnp.concatenate([v_imag, v_real], axis=-1),
        ],
        axis=1,
    )
    x_both = x_local.reshape(x_local.shape[0] * x_local.shape[1], x_local.shape[2])
    products = lax.dot_general(
        stacked, x_both, (((3,), (0,)), ((), ())), preferred_element_type=jnp.float32
    )
    slot_index = jnp.arange(v_local.shape[2], dtype=jnp.int32)
    live_slots = slot_index[None, None, :, None] < rank_local[:, None, None, None]
    return jnp.where(live_slots, products, jnp.float32(0.0)).astype(jnp.bfloat16)


def row_spectrum(u_local, blocks):
    products = lax.dot_general(
        u_local, blocks, (((0, 2), (0, 2)), ((), ())), preferred_element_type=jnp.float32
    )
    real_part = products[0, :, 0] - products[1, :, 1]
    imag_part = products[0, :, 1] + products[1, :, 0]
    return jnp.stack([real_part, imag_part], axis=0).astype(jnp.bfloat16)


def row_products(u_part, blocks):
    return lax.dot_general(
        u_part, blocks, (((0, 2), (0, 2)), ((), ())), preferred_element_type=jnp.float32
    )


def finish_spectrum(products):
    real_part = products[0, :, 0] - products[1, :, 1]
    imag_part = products[0, :, 1] + products[1, :, 0]
    return jnp.stack([real_part, imag_part], axis=0).astype(jnp.bfloat16)


def relay_exchange(own, u_local):
    t = lax.axis_index("tile")
    row = t // 2
    mine = lax.dynamic_index_in_dim(own, row, 0, keepdims=False)
    other = lax.dynamic_index_in_dim(own, 1 - row, 0, keepdims=False)
    pairs = [(0, 1), (1, 0), (2, 3), (3, 2)]
    across = lax.ppermute(other, "tile", [(0, 2), (2, 0), (1, 3), (3, 1)])
    partner = lax.ppermute(mine, "tile", pairs)
    passed = lax.ppermute(across, "tile", pairs)
    columns = (t, t ^ 2, t ^ 1, t ^ 3)
    u_order = [lax.dynamic_index_in_dim(u_local, j, 0, keepdims=False) for j in columns]
    early = row_products(
        jnp.stack(u_order[:3], axis=0), jnp.stack([mine, across, partner], axis=0)
    )
    last_u = u_order[3]

    def spectrum_of(start, width):
        u_part = lax.dynamic_slice_in_dim(last_u, start, width, axis=2)
        late = row_products(u_part[None], passed[None])
        return finish_spectrum(lax.dynamic_slice_in_dim(early, start, width, axis=1) + late)

    return spectrum_of


def gather_exchange(own, u_local, n_tile):
    repeat = n_tile // own.shape[0]
    sending = jnp.repeat(own, repeat, axis=0)
    received = lax.all_to_all(sending, "tile", split_axis=0, concat_axis=0, tiled=True)
    return row_spectrum(u_local, received)


def freq_exchange(spectrum_of, count_rec, n_freq):
    f = lax.axis_index("freq")
    width = count_rec // n_freq
    sent = {}
    for d in reversed(range(1, n_freq)):
        part = spectrum_of((f ^ d) * width, width)
        pairs = [(i, i ^ d) for i in range(n_freq)]
        sent[d] = lax.ppermute(part, "freq", pairs)
    pieces = [(f, spectrum_of(f * width, width))]
    pieces += [(f ^ d, sent[d]) for d in range(1, n_freq)]
    return pieces


def make_per_device(n_tile, n_freq):
    def per_device(sources, v_factors, u_factors, tile_ranks, window_bounds):
        v_local = v_factors[0, 0]
        u_local = u_factors[0]
        x_local = sources[0]
        rank_local = tile_ranks[0, :, 0]
        rows = v_local.shape[0]
        use_relay = n_tile == 4 and rows == 2 and u_local.shape[0] == 4
        use_swaps = n_freq & (n_freq - 1) == 0
        count_s = x_local.shape[2]
        chunks = S_CHUNKS if count_s % S_CHUNKS == 0 else 1
        width = count_s // chunks
        received_parts = []
        for c in range(chunks):
            x_part = x_local[:, :, c * width:(c + 1) * width]
            own = column_products(v_local, x_part, rank_local)
            if use_relay:
                spectrum_of = relay_exchange(own, u_local)
            else:
                spectrum = gather_exchange(own, u_local, n_tile)
                spectrum_of = lambda start, width, spectrum=spectrum: (
                    lax.dynamic_slice_in_dim(spectrum, start, width, axis=1)
                )
            if use_swaps:
                received_parts.append(freq_exchange(spectrum_of, u_local.shape[3], n_freq))
            else:
                spectrum = spectrum_of(0, u_local.shape[3])
                received = lax.all_to_all(
                    spectrum[None], "freq", split_axis=2, concat_axis=0, tiled=True
                )
                received_parts.append([(f, received[f]) for f in range(n_freq)])
        pieces = [
            (
                index,
                jnp.concatenate([part[k][1] for part in received_parts], axis=2)
                if chunks > 1
                else piece,
            )
            for k, (index, piece) in enumerate(received_parts[0])
        ]
        cosine_table, sine_table = inverse_tables(n_freq, NT)
        scale = 1.0 / math.sqrt(n_freq)
        count_s = window_bounds.shape[2]
        rows = []
        for index, _ in pieces:
            for table in (cosine_table, sine_table):
                row = lax.dynamic_index_in_dim(table, index, 0, keepdims=False) * scale
                rows.append(jnp.broadcast_to(row[:, None], (NT, count_s)))
        rows = lax.optimization_barrier(rows)
        traces = 0.0
        for k, (_, piece) in enumerate(pieces):
            widened = piece.astype(jnp.float32)
            traces = (
                traces
                + widened[0][:, None, :] * rows[2 * k][None]
                - widened[1][:, None, :] * rows[2 * k + 1][None]
            )
        time_index = jnp.arange(NT, dtype=jnp.int32)[None, :, None]
        inside = (time_index >= window_bounds[0][:, None, :]) & (
            time_index < window_bounds[1][:, None, :]
        )
        return jnp.where(inside, traces, jnp.float32(0.0))

    return per_device


def solution(mesh):
    return jax.shard_map(
        make_per_device(mesh.shape["tile"], mesh.shape["freq"]),
        mesh=mesh,
        in_specs=(
            P("freq", "grp", "tile", None),
            P("freq", "tile", None, "grp", None, None),
            P("freq", None, "grp", None, "tile"),
            P("freq", "grp", "tile"),
            P("grp", ("tile", "freq"), None),
        ),
        out_specs=P(("tile", "freq"), "grp", None),
        check_vma=False,
    )
```
